256 devices in a mesh: ctx: 16 (over x_lo, z), fsdp: 4 (over y), head: 4 (over x_hi, core).
Axes of the slice: x: 4 (x_hi: 2, x_lo: 2; x = x_hi * 2 + x_lo), y: 4, z: 8, core: 2. Of those that a mesh axis runs over, the one named last changes fastest.
Arguments:
- queries: bfloat16 [4, 8192, 2048], P('fsdp', 'ctx', 'head'), may hold values from -6 to 6
- keys: bfloat16 [4, 8192, 2048], P('fsdp', 'ctx', 'head'), may hold values from -6 to 6
- values: bfloat16 [4, 8192, 2048], P('fsdp', 'ctx', 'head'), may hold values from -6 to 6
- gate_pre: bfloat16 [4, 8192, 2048], P('fsdp', 'ctx', 'head'), may hold values from -6 to 6
- log_decay: float32 [4, 8192, 16], P('fsdp', 'ctx', 'head'), may hold values from -2 to 0, as said below
- out_grad: bfloat16 [4, 8192, 4096], P('fsdp', 'ctx', 'head'), may hold values from -6 to 6
- out_weight: float32 [4096, 2048], P(('ctx', 'fsdp'), 'head'), may hold values from -0.125 to 0.125
- moment_one: float32 [4096, 2048], P(('ctx', 'fsdp'), 'head'), may hold values from -2 to 2
- moment_two: float32 [4096, 2048], P(('ctx', 'fsdp'), 'head'), may hold values from 0.05 to 1
- group_ids: int32 [128], P(('ctx', 'fsdp')), may hold values from 0 to 2
- step_count: int32 [1], replicated, may hold values from 1 to 40
Outputs:
- query_grad: bfloat16 [4, 8192, 2048], P('fsdp', 'ctx', 'head')
- key_grad: bfloat16 [4, 8192, 2048], P('fsdp', 'ctx', 'head')
- value_grad: bfloat16 [4, 8192, 2048], P('fsdp', 'ctx', 'head')
- new_moment_one: float32 [4096, 2048], P(('ctx', 'fsdp'), 'head')
- new_moment_two: float32 [4096, 2048], P(('ctx', 'fsdp'), 'head')
- weight_step: float32 [4096, 2048], P(('ctx', 'fsdp'), 'head')
The draws below stay inside these ranges and needn't reach their ends.
Inputs may be any that keep to these rules, and one draw needn't show every extreme that they name: `log_decay`: Log-decays per token and head, never positive. `group_ids`: 0 for a frozen block of rows, 1 for one updated without weight decay, 2 for one updated with it.
All inputs are finite; a program needn't handle non-finite values.
Results may differ from the reference program's by a relative error of at most 0.017.
Values may be sent and summed in bfloat16 or wider, within the bound.
No kernel may reach another device: no remote copies, remote signals or barrier semaphores. Data moves between devices by JAX's collectives and lax.ppermute only.
A program may use at most 128 MiB of HBM per device.

```python
import math
import jax
import jax.numpy as jnp
from jax import lax

D = 4096
HEADS = 16
HEAD_DIM = 128
SPAN = 256
ROW_BLOCK = 32
SEQS = 4
LEN = 8192
HW = 2048


def draw_log_decay(key, part):
    streams = jax.random.split(key, 7)
    share = 0.5
    quick = jax.random.uniform(streams[0], (SEQS, 1, HEADS)) < share
    window = max(SPAN, 64) * jax.random.uniform(streams[1], (SEQS, 1, HEADS), minval=0.12, maxval=0.2)
    quick_rate = 2.302585 / window
    steady_rate = jax.random.uniform(streams[2], (SEQS, 1, HEADS), minval=0.1, maxval=0.5) / LEN
    base_rate = jnp.where(quick, quick_rate, steady_rate)
    rough = jax.random.uniform(streams[3], (SEQS, LEN, HEADS), minval=0.5, maxval=1.5)
    block_factor = jax.random.uniform(streams[4], (SEQS, LEN // SPAN, 1, HEADS), minval=0.5, maxval=1.5)
    block_factor = jnp.broadcast_to(block_factor, (SEQS, LEN // SPAN, SPAN, HEADS)).reshape(SEQS, LEN, HEADS)
    places = jax.random.randint(streams[5], (SEQS, 3, HEADS), 0, LEN)
    positions = jnp.arange(LEN)
    bursting = jnp.any(positions[None, :, None, None] == places[:, None, :, :], axis=2)
    sudden = jnp.log(jax.random.uniform(streams[6], (SEQS, LEN, HEADS), minval=0.6, maxval=0.8))
    smooth = -base_rate * rough * block_factor
    return jnp.where(bursting, smooth + sudden, smooth).astype(jnp.float32)


def with_ends(drawn, rng, low, top_value):
    dims = drawn.shape
    place = [jax.random.randint(jax.random.fold_in(rng, axis), (), 0, dims[axis]) for axis in range(len(dims))]
    drawn = drawn.at[tuple(place)].set(low)
    longest = dims.index(max(dims))
    place[longest] = (place[longest] + 1) % dims[longest]
    return drawn.at[tuple(place)].set(top_value)


def strengthened(drawn, key, source, target, parts, factor):
    def block_of(axis_at):
        return (jnp.arange(drawn.shape[axis_at]) // (drawn.shape[axis_at] // parts)).reshape((-1,) + (1,) * (drawn.ndim - 1 - axis_at))

    near = jax.random.permutation(key, parts)[block_of(target)]
    second = (block_of(target) + parts // 2) % parts
    return jnp.where((block_of(source) == near) | (block_of(source) == second), factor * drawn, drawn)


def level_of(stream_key, dims, pieces, least, largest):
    def one(position, blocks):
        steps = jax.random.uniform(jax.random.fold_in(jax.random.fold_in(stream_key, 6), position), (blocks,), jnp.float32, least / len(pieces), largest / len(pieces))
        return jnp.repeat(jnp.exp(steps), dims[position] // blocks).reshape((-1,) + (1,) * (len(dims) - position - 1))

    gain = one(*pieces[0])
    for cut in pieces[1:]:
        gain = gain * one(*cut)
    return gain


def noise(key, extent, deviation, most, cuts=(), kind=jnp.bfloat16):
    result = deviation * jax.random.normal(key, extent, jnp.float32)
    if cuts:
        result = result * level_of(key, extent, cuts, -0.22, 0.18)
    return jnp.clip(result, -most, most).astype(kind)


def bell_draw_with(own_key, extent, width, most, shards, heavy, kind=jnp.bfloat16):
    result = width * jax.random.normal(own_key, extent, jnp.float32)
    if shards:
        result = result * level_of(own_key, extent, shards, -0.22, 0.18)
    return jnp.clip(strengthened(result, jax.random.fold_in(own_key, 3), *heavy), -most, most).astype(kind)


def setup_inputs(seed: int = 0) -> dict:
    splits = jax.random.split(jax.random.key(seed), 12)
    queries = noise(splits[0], (SEQS, LEN, HW), 1.0, 6.0, ((0, 4), (1, 16), (2, 4)))
    keys = noise(splits[1], (SEQS, LEN, HW), 1.0, 6.0, ((0, 4), (1, 16), (2, 4)))
    values = noise(splits[2], (SEQS, LEN, HW), 1.0, 6.0, ((0, 4), (1, 16), (2, 4)))
    gate_pre = noise(splits[3], (SEQS, LEN, HW), 1.0, 6.0, ((0, 4), (1, 16), (2, 4)))
    log_decay = draw_log_decay(jax.random.fold_in(splits[11], 71), 0)
    out_grad = bell_draw_with(splits[5], (SEQS, LEN, D), 1.0, 6.0, ((0, 4), (1, 16), (2, 4)), (1, 2, 16, 2.0))
    out_weight = noise(splits[6], (D, HW), HW ** -0.5, 0.125, ((0, 64), (1, 4)), jnp.float32)
    moment_one = noise(splits[7], (D, HW), 0.3, 2.0, ((0, 64), (1, 4)), jnp.float32)
    moment_two = jnp.clip(jnp.exp(math.log(1.0) - 2.9957323 * jax.random.uniform(splits[8], (D, HW), jnp.float32) ** level_of(splits[8], (D, HW), ((0, 64), (1, 4)), -0.2, 0.2)), 0.05, 1.0)
    group_ids = with_ends(jax.random.randint(splits[9], (D // ROW_BLOCK,), 0, 3), jax.random.fold_in(splits[9], 1), 0, 2).astype(jnp.int32)
    step_count = jax.random.randint(splits[10], (1,), 1, 41).astype(jnp.int32)
    return dict(queries=queries, keys=keys, values=values, gate_pre=gate_pre, log_decay=log_decay, out_grad=out_grad, out_weight=out_weight, moment_one=moment_one, moment_two=moment_two, group_ids=group_ids, step_count=step_count)


NORM_EPS = 1e-06
BETA_ONE = 0.9
BETA_TWO = 0.95
ADAM_EPS = 1e-08
WEIGHT_DECAY = 0.1

def to_blocks(array):
    shape = array.shape
    grouped = array.reshape((shape[0], shape[1] // SPAN, SPAN) + shape[2:])
    return jnp.moveaxis(grouped, 1, 0)

def from_blocks(array):
    moved = jnp.moveaxis(array, 0, 1)
    shape = moved.shape
    return moved.reshape((shape[0], shape[1] * shape[2]) + shape[3:])

def decay_mask(cumul):
    along = jnp.swapaxes(cumul, 1, 2)
    spread = along[:, :, :, None] - along[:, :, None, :]
    length = cumul.shape[1]
    lower = jnp.tril(jnp.ones((length, length), jnp.float32))
    return jnp.exp(jnp.minimum(spread, 0.0)) * lower

def reference(queries, keys, values, gate_pre, log_decay, out_grad, out_weight, moment_one, moment_two, group_ids, step_count):
    shaped = (SEQS, LEN, HEADS, HEAD_DIM)
    query_blocks = to_blocks(queries.reshape(shaped))
    key_blocks = to_blocks(keys.reshape(shaped))
    value_blocks = to_blocks(values.reshape(shaped))
    cumul = jnp.cumsum(to_blocks(log_decay), axis=2)
    totals = cumul[:, :, -1, :]

    def forward(state, item):
        query_c, key_c, value_c, cumul_c, total_c = item
        masking = decay_mask(cumul_c)
        scores = jnp.einsum('sthe,suhe->shtu', query_c.astype(jnp.float32), key_c.astype(jnp.float32))
        probs = (scores * masking).astype(jnp.bfloat16)
        intra = jnp.einsum('shtu,suhe->sthe', probs.astype(jnp.float32), value_c.astype(jnp.float32))
        rounded = state.astype(jnp.bfloat16)
        inter = jnp.exp(cumul_c)[..., None] * jnp.einsum('sthe,shef->sthf', query_c.astype(jnp.float32), rounded.astype(jnp.float32))
        scaled = (jnp.exp(total_c[:, None, :] - cumul_c)[..., None] * key_c.astype(jnp.float32)).astype(jnp.bfloat16)
        update = jnp.einsum('sthe,sthf->shef', scaled.astype(jnp.float32), value_c.astype(jnp.float32))
        state = jnp.exp(total_c)[:, :, None, None] * state + update
        return (state, (intra + inter, rounded))
    initial = jnp.zeros((SEQS, HEADS, HEAD_DIM, HEAD_DIM), jnp.float32)
    _, (attn_blocks, state_list) = lax.scan(forward, initial, (query_blocks, key_blocks, value_blocks, cumul, totals))
    attn = from_blocks(attn_blocks)
    square = lax.optimization_barrier(jnp.mean(attn * attn, axis=-1, keepdims=True))
    inverse = lax.rsqrt(square + NORM_EPS)
    normed = attn * inverse
    silu_gate = jax.nn.silu(gate_pre.reshape(shaped).astype(jnp.float32))
    mixed = (normed * silu_gate).astype(jnp.bfloat16).reshape(SEQS * LEN, HW)
    flat_grad = out_grad.reshape(SEQS * LEN, D)
    weight_b = out_weight.astype(jnp.bfloat16)
    mixed_grad = jnp.dot(flat_grad, weight_b, preferred_element_type=jnp.float32).reshape(shaped)
    weight_grad = jnp.dot(flat_grad.T, mixed, preferred_element_type=jnp.float32)
    normed_grad = mixed_grad * silu_gate
    inner = lax.optimization_barrier(jnp.mean(normed_grad * normed, axis=-1, keepdims=True))
    attn_grad = (inverse * (normed_grad - normed * inner)).astype(jnp.bfloat16)
    grad_blocks = to_blocks(attn_grad)

    def backward(carry, item):
        query_c, key_c, value_c, agrad_c, cumul_c, total_c, rounded = item
        masking = decay_mask(cumul_c)
        query_f = query_c.astype(jnp.float32)
        key_f = key_c.astype(jnp.float32)
        value_f = value_c.astype(jnp.float32)
        agrad_f = agrad_c.astype(jnp.float32)
        scores = jnp.einsum('sthe,suhe->shtu', query_f, key_f)
        probs = (scores * masking).astype(jnp.bfloat16).astype(jnp.float32)
        inners = jnp.einsum('sthf,suhf->shtu', agrad_f, value_f)
        dprobs = (inners * masking).astype(jnp.bfloat16).astype(jnp.float32)
        back_b = carry.astype(jnp.bfloat16).astype(jnp.float32)
        decay_in = jnp.exp(cumul_c)[..., None]
        decay_out = jnp.exp(total_c[:, None, :] - cumul_c)[..., None]
        qgrad = jnp.einsum('shtu,suhe->sthe', dprobs, key_f) + decay_in * jnp.einsum('sthf,shef->sthe', agrad_f, rounded.astype(jnp.float32))
        kgrad = jnp.einsum('shtu,sthe->suhe', dprobs, query_f) + decay_out * jnp.einsum('suhf,shef->suhe', value_f, back_b)
        vgrad = jnp.einsum('shtu,sthf->suhf', probs, agrad_f) + decay_out * jnp.einsum('suhe,shef->suhf', key_f, back_b)
        weighted = (decay_in * query_f).astype(jnp.bfloat16).astype(jnp.float32)
        carry = jnp.exp(total_c)[:, :, None, None] * carry + jnp.einsum('sthe,sthf->shef', weighted, agrad_f)
        return (carry, (qgrad.astype(jnp.bfloat16), kgrad.astype(jnp.bfloat16), vgrad.astype(jnp.bfloat16)))
    _, (qgrad_b, kgrad_b, vgrad_b) = lax.scan(backward, initial, (query_blocks, key_blocks, value_blocks, grad_blocks, cumul, totals, state_list), reverse=True)
    query_grad = from_blocks(qgrad_b).reshape(SEQS, LEN, HW)
    key_grad = from_blocks(kgrad_b).reshape(SEQS, LEN, HW)
    value_grad = from_blocks(vgrad_b).reshape(SEQS, LEN, HW)
    grad = weight_grad / jnp.sqrt(jnp.float32(SEQS * LEN))
    row_group = jnp.repeat(group_ids, ROW_BLOCK)[:, None]
    stepped = step_count[0].astype(jnp.float32)
    first = BETA_ONE * moment_one + (1.0 - BETA_ONE) * grad
    second = BETA_TWO * moment_two + (1.0 - BETA_TWO) * grad * grad
    correct_one = 1.0 - jnp.power(BETA_ONE, stepped)
    correct_two = 1.0 - jnp.power(BETA_TWO, stepped)
    active = row_group >= 1
    decayed = (row_group == 2).astype(jnp.float32)
    direction = first / correct_one / (jnp.sqrt(second / correct_two) + ADAM_EPS) + WEIGHT_DECAY * decayed * out_weight
    new_moment_one = jnp.where(active, first, moment_one)
    new_moment_two = jnp.where(active, second, moment_two)
    weight_step = jnp.where(active, direction, 0.0)
    return (query_grad, key_grad, value_grad, new_moment_one, new_moment_two, weight_step)
```

```python
import jax
import jax.numpy as jnp
from jax import lax
from jax.sharding import PartitionSpec as P

HEAD_DIM = 128
SPAN = 256
ROW_BLOCK = 32


NORM_EPS = 1e-06
BETA_ONE = 0.9
BETA_TWO = 0.95
ADAM_EPS = 1e-08
WEIGHT_DECAY = 0.1


def prefix_scan(gain, state, axis):
    count = lax.axis_size(axis)
    place = lax.axis_index(axis)
    gain, state = lax.ppermute((gain, state), axis, [(i, i + 1) for i in range(count - 1)])
    gain = jnp.where(place >= 1, gain, 1.0)
    step = 1
    while step < count:
        got_gain, got_state = lax.ppermute(
            (gain, state), axis, [(i, i + step) for i in range(count - step)]
        )
        reached = place >= step
        state = jnp.where(reached, gain[:, None, None] * got_state + state, state)
        gain = jnp.where(reached, got_gain * gain, gain)
        step *= 2
    return state


def suffix_scan(gain, state, axis):
    count = lax.axis_size(axis)
    place = lax.axis_index(axis)
    gain, state = lax.ppermute((gain, state), axis, [(i + 1, i) for i in range(count - 1)])
    gain = jnp.where(place <= count - 2, gain, 1.0)
    step = 1
    while step < count:
        got_gain, got_state = lax.ppermute(
            (gain, state), axis, [(i + step, i) for i in range(count - step)]
        )
        reached = place + step <= count - 1
        state = jnp.where(reached, state + gain[:, None, None] * got_state, state)
        gain = jnp.where(reached, gain * got_gain, gain)
        step *= 2
    return state


def decay_mask(cumul):
    along = jnp.swapaxes(cumul, 1, 2)
    spread = along[:, :, :, None] - along[:, :, None, :]
    length = cumul.shape[1]
    lower = jnp.tril(jnp.ones((length, length), jnp.float32))
    return jnp.exp(jnp.minimum(spread, 0.0)) * lower


def per_device(
    queries,
    keys,
    values,
    gate_pre,
    log_decay,
    out_grad,
    out_weight,
    moment_one,
    moment_two,
    group_ids,
    step_count,
):
    tok_local = queries.shape[1]
    head_local = log_decay.shape[2]
    width_local = queries.shape[2]
    blocks = tok_local // SPAN
    shaped = (blocks, SPAN, head_local, HEAD_DIM)
    query_c = queries.reshape(shaped)
    key_c = keys.reshape(shaped)
    value_c = values.reshape(shaped)
    cumul = jnp.cumsum(log_decay.reshape(blocks, SPAN, head_local), axis=1)
    totals = cumul[:, -1, :]
    masking = decay_mask(cumul)
    decay_in = jnp.exp(cumul)[..., None]
    decay_out = jnp.exp(totals[:, None, :] - cumul)[..., None]
    scores = jnp.einsum("cthe,cuhe->chtu", query_c, key_c, preferred_element_type=jnp.float32)
    probs = (scores * masking).astype(jnp.bfloat16)
    intra = jnp.einsum("chtu,cuhe->cthe", probs, value_c, preferred_element_type=jnp.float32)
    scaled = (decay_out * key_c).astype(jnp.bfloat16)
    updates = jnp.einsum("cthe,cthf->chef", scaled, value_c, preferred_element_type=jnp.float32)
    running = jnp.zeros((head_local, HEAD_DIM, HEAD_DIM), jnp.float32)
    leading = jnp.zeros((head_local,), jnp.float32)
    start_list = []
    lead_list = []
    for block in range(blocks):
        start_list.append(running)
        lead_list.append(leading)
        running = jnp.exp(totals[block])[:, None, None] * running + updates[block]
        leading = leading + totals[block]
    local_start = jnp.stack(start_list)
    lead_sums = jnp.stack(lead_list)
    incoming = prefix_scan(jnp.exp(leading), running, "ctx")
    states = local_start + jnp.exp(lead_sums)[:, :, None, None] * incoming[None]
    rounded = states.astype(jnp.bfloat16)
    inter = decay_in * jnp.einsum(
        "cthe,chef->cthf", query_c, rounded, preferred_element_type=jnp.float32
    )
    attn = intra + inter
    square = jnp.mean(attn * attn, axis=-1, keepdims=True)
    inverse = lax.rsqrt(square + NORM_EPS)
    normed = attn * inverse
    silu_gate = jax.nn.silu(gate_pre.reshape(shaped).astype(jnp.float32))
    mixed = (normed * silu_gate).astype(jnp.bfloat16).reshape(tok_local, width_local)
    features = lax.all_gather(out_grad, "head", axis=2, tiled=True)[0]
    weight_b = out_weight.astype(jnp.bfloat16)
    columns = features
    mixed_grad = jnp.dot(
        columns,
        lax.all_gather(
            lax.all_gather(weight_b, "fsdp", axis=0, tiled=True), "ctx", axis=0, tiled=True
        ),
        preferred_element_type=jnp.float32,
    )
    columns = features
    grad_rows = lax.psum_scatter(
        lax.psum_scatter(
            jnp.einsum("td,th->dh", columns, mixed, preferred_element_type=jnp.float32),
            "ctx",
            scatter_dimension=0,
            tiled=True,
        ),
        "fsdp",
        scatter_dimension=0,
        tiled=True,
    )
    normed_grad = mixed_grad.reshape(shaped) * silu_gate
    inner = jnp.mean(normed_grad * normed, axis=-1, keepdims=True)
    attn_grad = (inverse * (normed_grad - normed * inner)).astype(jnp.bfloat16)
    inners = jnp.einsum("cthf,cuhf->chtu", attn_grad, value_c, preferred_element_type=jnp.float32)
    dprobs = (inners * masking).astype(jnp.bfloat16)
    qgrad = jnp.einsum("chtu,cuhe->cthe", dprobs, key_c, preferred_element_type=jnp.float32)
    kgrad = jnp.einsum("chtu,cthe->cuhe", dprobs, query_c, preferred_element_type=jnp.float32)
    vgrad = jnp.einsum("chtu,cthf->cuhf", probs, attn_grad, preferred_element_type=jnp.float32)
    weighted = (decay_in * query_c).astype(jnp.bfloat16)
    back_updates = jnp.einsum(
        "cthe,cthf->chef", weighted, attn_grad, preferred_element_type=jnp.float32
    )
    backing = jnp.zeros((head_local, HEAD_DIM, HEAD_DIM), jnp.float32)
    trailing = jnp.zeros((head_local,), jnp.float32)
    after_list = [None] * blocks
    trail_list = [None] * blocks
    for block in reversed(range(blocks)):
        after_list[block] = backing
        trail_list[block] = trailing
        backing = jnp.exp(totals[block])[:, None, None] * backing + back_updates[block]
        trailing = trailing + totals[block]
    local_after = jnp.stack(after_list)
    trail_sums = jnp.stack(trail_list)
    arriving = suffix_scan(jnp.exp(leading), backing, "ctx")
    after_full = local_after + jnp.exp(trail_sums)[:, :, None, None] * arriving[None]
    back_b = after_full.astype(jnp.bfloat16)
    qgrad = qgrad + decay_in * jnp.einsum(
        "cthf,chef->cthe", attn_grad, rounded, preferred_element_type=jnp.float32
    )
    kgrad = kgrad + decay_out * jnp.einsum(
        "cuhf,chef->cuhe", value_c, back_b, preferred_element_type=jnp.float32
    )
    vgrad = vgrad + decay_out * jnp.einsum(
        "cuhe,chef->cuhf", key_c, back_b, preferred_element_type=jnp.float32
    )
    query_grad = qgrad.astype(jnp.bfloat16).reshape(1, tok_local, width_local)
    key_grad = kgrad.astype(jnp.bfloat16).reshape(1, tok_local, width_local)
    value_grad = vgrad.astype(jnp.bfloat16).reshape(1, tok_local, width_local)
    token_count = tok_local * lax.axis_size("ctx") * lax.axis_size("fsdp")
    grad = grad_rows / jnp.sqrt(jnp.float32(token_count))
    row_group = jnp.repeat(group_ids, ROW_BLOCK)[:, None]
    stepped = step_count[0].astype(jnp.float32)
    first = BETA_ONE * moment_one + (1.0 - BETA_ONE) * grad
    second = BETA_TWO * moment_two + (1.0 - BETA_TWO) * grad * grad
    correct_one = 1.0 - jnp.power(BETA_ONE, stepped)
    correct_two = 1.0 - jnp.power(BETA_TWO, stepped)
    active = row_group >= 1
    decayed = (row_group == 2).astype(jnp.float32)
    direction = (
        first / correct_one / (jnp.sqrt(second / correct_two) + ADAM_EPS)
        + WEIGHT_DECAY * decayed * out_weight
    )
    new_moment_one = jnp.where(active, first, moment_one)
    new_moment_two = jnp.where(active, second, moment_two)
    weight_step = jnp.where(active, direction, 0.0)
    return (query_grad, key_grad, value_grad, new_moment_one, new_moment_two, weight_step)


def solution(mesh):
    in_specs = (
        P("fsdp", "ctx", "head"),
        P("fsdp", "ctx", "head"),
        P("fsdp", "ctx", "head"),
        P("fsdp", "ctx", "head"),
        P("fsdp", "ctx", "head"),
        P("fsdp", "ctx", "head"),
        P(("ctx", "fsdp"), "head"),
        P(("ctx", "fsdp"), "head"),
        P(("ctx", "fsdp"), "head"),
        P(("ctx", "fsdp")),
        P(),
    )
    out_specs = (
        P("fsdp", "ctx", "head"),
        P("fsdp", "ctx", "head"),
        P("fsdp", "ctx", "head"),
        P(("ctx", "fsdp"), "head"),
        P(("ctx", "fsdp"), "head"),
        P(("ctx", "fsdp"), "head"),
    )
    return jax.shard_map(
        per_device, mesh=mesh, in_specs=in_specs, out_specs=out_specs, check_vma=False
    )
```

```python
import jax
import jax.numpy as jnp
from jax import lax
from jax.sharding import PartitionSpec as P

HEAD_DIM = 128
SPAN = 256
ROW_BLOCK = 32


NORM_EPS = 1e-06
BETA_ONE = 0.9
BETA_TWO = 0.95
ADAM_EPS = 1e-08
WEIGHT_DECAY = 0.1


def window_scan(gain, state, axis, sign):
    count = lax.axis_size(axis)
    place = lax.axis_index(axis)

    def join(near, far):
        return (near[0] * far[0], near[1] + near[0][:, None, None] * far[1])

    def fetch(value, step):
        pairs = [(i, i + sign * step) for i in range(count) if 0 <= i + sign * step < count]
        got = lax.ppermute(value, axis, pairs)
        source = place - sign * step
        present = (source >= 0) & (source < count)
        return jax.tree.map(lambda g, e: jnp.where(present, g, e), got, identity)

    own = (gain, state)
    identity = (jnp.ones_like(gain), jnp.zeros_like(state))
    near = [fetch(own, step) for step in (1, 2, 3)]
    inner = join(join(near[0], near[1]), near[2])
    window = join(own, inner)
    total = inner
    for step in (4, 8, 12):
        total = join(total, fetch(window, step))
    return total[1]


def decay_mask(cumul):
    along = jnp.swapaxes(cumul, 1, 2)
    spread = along[:, :, :, None] - along[:, :, None, :]
    length = cumul.shape[1]
    lower = jnp.tril(jnp.ones((length, length), jnp.float32))
    return jnp.exp(jnp.minimum(spread, 0.0)) * lower


def per_device(
    queries,
    keys,
    values,
    gate_pre,
    log_decay,
    out_grad,
    out_weight,
    moment_one,
    moment_two,
    group_ids,
    step_count,
):
    tok_local = queries.shape[1]
    head_local = log_decay.shape[2]
    width_local = queries.shape[2]
    blocks = tok_local // SPAN
    shaped = (blocks, SPAN, head_local, HEAD_DIM)
    query_c = queries.reshape(shaped)
    key_c = keys.reshape(shaped)
    value_c = values.reshape(shaped)
    cumul = jnp.cumsum(log_decay.reshape(blocks, SPAN, head_local), axis=1)
    totals = cumul[:, -1, :]
    masking = decay_mask(cumul)
    decay_in = jnp.exp(cumul)[..., None]
    decay_out = jnp.exp(totals[:, None, :] - cumul)[..., None]
    scores = jnp.einsum("cthe,cuhe->chtu", query_c, key_c, preferred_element_type=jnp.float32)
    probs = (scores * masking).astype(jnp.bfloat16)
    intra = jnp.einsum("chtu,cuhe->cthe", probs, value_c, preferred_element_type=jnp.float32)
    scaled = (decay_out * key_c).astype(jnp.bfloat16)
    updates = jnp.einsum("cthe,cthf->chef", scaled, value_c, preferred_element_type=jnp.float32)
    running = jnp.zeros((head_local, HEAD_DIM, HEAD_DIM), jnp.float32)
    leading = jnp.zeros((head_local,), jnp.float32)
    start_list = []
    lead_list = []
    for block in range(blocks):
        start_list.append(running)
        lead_list.append(leading)
        running = jnp.exp(totals[block])[:, None, None] * running + updates[block]
        leading = leading + totals[block]
    local_start = jnp.stack(start_list)
    lead_sums = jnp.stack(lead_list)
    incoming = window_scan(jnp.exp(leading), running, "ctx", 1)
    states = local_start + jnp.exp(lead_sums)[:, :, None, None] * incoming[None]
    rounded = states.astype(jnp.bfloat16)
    inter = decay_in * jnp.einsum(
        "cthe,chef->cthf", query_c, rounded, preferred_element_type=jnp.float32
    )
    attn = intra + inter
    square = jnp.mean(attn * attn, axis=-1, keepdims=True)
    inverse = lax.rsqrt(square + NORM_EPS)
    normed = attn * inverse
    silu_gate = jax.nn.silu(gate_pre.reshape(shaped).astype(jnp.float32))
    mixed = (normed * silu_gate).astype(jnp.bfloat16).reshape(tok_local, width_local)
    features = lax.all_gather(out_grad, "head", axis=2, tiled=True)[0]
    weight_b = out_weight.astype(jnp.bfloat16)
    columns = features
    mixed_grad = jnp.dot(
        columns,
        lax.all_gather(
            lax.all_gather(weight_b, "fsdp", axis=0, tiled=True), "ctx", axis=0, tiled=True
        ),
        preferred_element_type=jnp.float32,
    )
    columns = features
    grad_rows = lax.psum_scatter(
        lax.psum_scatter(
            jnp.einsum("td,th->dh", columns, mixed, preferred_element_type=jnp.float32).astype(
                jnp.bfloat16
            ),
            "ctx",
            scatter_dimension=0,
            tiled=True,
        ).astype(jnp.float32),
        "fsdp",
        scatter_dimension=0,
        tiled=True,
    )
    normed_grad = mixed_grad.reshape(shaped) * silu_gate
    inner = jnp.mean(normed_grad * normed, axis=-1, keepdims=True)
    attn_grad = (inverse * (normed_grad - normed * inner)).astype(jnp.bfloat16)
    inners = jnp.einsum("cthf,cuhf->chtu", attn_grad, value_c, preferred_element_type=jnp.float32)
    dprobs = (inners * masking).astype(jnp.bfloat16)
    qgrad = jnp.einsum("chtu,cuhe->cthe", dprobs, key_c, preferred_element_type=jnp.float32)
    kgrad = jnp.einsum("chtu,cthe->cuhe", dprobs, query_c, preferred_element_type=jnp.float32)
    vgrad = jnp.einsum("chtu,cthf->cuhf", probs, attn_grad, preferred_element_type=jnp.float32)
    weighted = (decay_in * query_c).astype(jnp.bfloat16)
    back_updates = jnp.einsum(
        "cthe,cthf->chef", weighted, attn_grad, preferred_element_type=jnp.float32
    )
    backing = jnp.zeros((head_local, HEAD_DIM, HEAD_DIM), jnp.float32)
    trailing = jnp.zeros((head_local,), jnp.float32)
    after_list = [None] * blocks
    trail_list = [None] * blocks
    for block in reversed(range(blocks)):
        after_list[block] = backing
        trail_list[block] = trailing
        backing = jnp.exp(totals[block])[:, None, None] * backing + back_updates[block]
        trailing = trailing + totals[block]
    local_after = jnp.stack(after_list)
    trail_sums = jnp.stack(trail_list)
    arriving = window_scan(jnp.exp(leading), backing, "ctx", -1)
    after_full = local_after + jnp.exp(trail_sums)[:, :, None, None] * arriving[None]
    back_b = after_full.astype(jnp.bfloat16)
    qgrad = qgrad + decay_in * jnp.einsum(
        "cthf,chef->cthe", attn_grad, rounded, preferred_element_type=jnp.float32
    )
    kgrad = kgrad + decay_out * jnp.einsum(
        "cuhf,chef->cuhe", value_c, back_b, preferred_element_type=jnp.float32
    )
    vgrad = vgrad + decay_out * jnp.einsum(
        "cuhe,chef->cuhf", key_c, back_b, preferred_element_type=jnp.float32
    )
    query_grad = qgrad.astype(jnp.bfloat16).reshape(1, tok_local, width_local)
    key_grad = kgrad.astype(jnp.bfloat16).reshape(1, tok_local, width_local)
    value_grad = vgrad.astype(jnp.bfloat16).reshape(1, tok_local, width_local)
    token_count = tok_local * lax.axis_size("ctx") * lax.axis_size("fsdp")
    grad = grad_rows / jnp.sqrt(jnp.float32(token_count))
    row_group = jnp.repeat(group_ids, ROW_BLOCK)[:, None]
    stepped = step_count[0].astype(jnp.float32)
    first = BETA_ONE * moment_one + (1.0 - BETA_ONE) * grad
    second = BETA_TWO * moment_two + (1.0 - BETA_TWO) * grad * grad
    correct_one = 1.0 - jnp.power(BETA_ONE, stepped)
    correct_two = 1.0 - jnp.power(BETA_TWO, stepped)
    active = row_group >= 1
    decayed = (row_group == 2).astype(jnp.float32)
    direction = (
        first / correct_one / (jnp.sqrt(second / correct_two) + ADAM_EPS)
        + WEIGHT_DECAY * decayed * out_weight
    )
    new_moment_one = jnp.where(active, first, moment_one)
    new_moment_two = jnp.where(active, second, moment_two)
    weight_step = jnp.where(active, direction, 0.0)
    return (query_grad, key_grad, value_grad, new_moment_one, new_moment_two, weight_step)


def solution(mesh):
    in_specs = (
        P("fsdp", "ctx", "head"),
        P("fsdp", "ctx", "head"),
        P("fsdp", "ctx", "head"),
        P("fsdp", "ctx", "head"),
        P("fsdp", "ctx", "head"),
        P("fsdp", "ctx", "head"),
        P(("ctx", "fsdp"), "head"),
        P(("ctx", "fsdp"), "head"),
        P(("ctx", "fsdp"), "head"),
        P(("ctx", "fsdp")),
        P(),
    )
    out_specs = (
        P("fsdp", "ctx", "head"),
        P("fsdp", "ctx", "head"),
        P("fsdp", "ctx", "head"),
        P(("ctx", "fsdp"), "head"),
        P(("ctx", "fsdp"), "head"),
        P(("ctx", "fsdp"), "head"),
    )
    return jax.shard_map(
        per_device, mesh=mesh, in_specs=in_specs, out_specs=out_specs, check_vma=False
    )
```

```python
import jax
import jax.numpy as jnp
from jax import lax
from jax.sharding import PartitionSpec as P

HEAD_DIM = 128
SPAN = 256
ROW_BLOCK = 32


NORM_EPS = 1e-06
BETA_ONE = 0.9
BETA_TWO = 0.95
ADAM_EPS = 1e-08
WEIGHT_DECAY = 0.1


def window_scan(gain, state, axis, sign):
    count = lax.axis_size(axis)
    place = lax.axis_index(axis)

    def join(near, far):
        return (near[0] * far[0], near[1] + near[0][:, None, None] * far[1])

    def fetch(value, step):
        high = value[0].astype(jnp.bfloat16)
        low = (value[0] - high.astype(jnp.float32)).astype(jnp.bfloat16)
        extra = jnp.broadcast_to(jnp.stack([high, low], axis=1)[:, :, None], (value[1].shape[0], 2, value[1].shape[2]))
        packed = jnp.concatenate([value[1].astype(jnp.bfloat16), extra], axis=1)
        pairs = [(i, i + sign * step) for i in range(count) if 0 <= i + sign * step < count]
        got = lax.ppermute(packed, axis, pairs).astype(jnp.float32)
        rows = value[1].shape[1]
        got = (got[:, rows, 0] + got[:, rows + 1, 0], got[:, :rows])
        source = place - sign * step
        present = (source >= 0) & (source < count)
        return jax.tree.map(lambda g, e: jnp.where(present, g, e), got, identity)

    own = (gain, state)
    identity = (jnp.ones_like(gain), jnp.zeros_like(state))
    near = [fetch(own, step) for step in (1, 2, 3)]
    inner = join(join(near[0], near[1]), near[2])
    window = join(own, inner)
    total = inner
    for step in (4, 8, 12):
        total = join(total, fetch(window, step))
    return total[1]


def decay_mask(cumul):
    along = jnp.swapaxes(cumul, 1, 2)
    spread = along[:, :, :, None] - along[:, :, None, :]
    length = cumul.shape[1]
    lower = jnp.tril(jnp.ones((length, length), jnp.float32))
    return jnp.exp(jnp.minimum(spread, 0.0)) * lower


def per_device(
    queries,
    keys,
    values,
    gate_pre,
    log_decay,
    out_grad,
    out_weight,
    moment_one,
    moment_two,
    group_ids,
    step_count,
):
    tok_local = queries.shape[1]
    head_local = log_decay.shape[2]
    width_local = queries.shape[2]
    blocks = tok_local // SPAN
    shaped = (blocks, SPAN, head_local, HEAD_DIM)
    query_c = queries.reshape(shaped)
    key_c = keys.reshape(shaped)
    value_c = values.reshape(shaped)
    cumul = jnp.cumsum(log_decay.reshape(blocks, SPAN, head_local), axis=1)
    totals = cumul[:, -1, :]
    masking = decay_mask(cumul)
    decay_in = jnp.exp(cumul)[..., None]
    decay_out = jnp.exp(totals[:, None, :] - cumul)[..., None]
    scores = jnp.einsum("cthe,cuhe->chtu", query_c, key_c, preferred_element_type=jnp.float32)
    probs = (scores * masking).astype(jnp.bfloat16)
    intra = jnp.einsum("chtu,cuhe->cthe", probs, value_c, preferred_element_type=jnp.float32)
    scaled = (decay_out * key_c).astype(jnp.bfloat16)
    updates = jnp.einsum("cthe,cthf->chef", scaled, value_c, preferred_element_type=jnp.float32)
    running = jnp.zeros((head_local, HEAD_DIM, HEAD_DIM), jnp.float32)
    leading = jnp.zeros((head_local,), jnp.float32)
    start_list = []
    lead_list = []
    for block in range(blocks):
        start_list.append(running)
        lead_list.append(leading)
        running = jnp.exp(totals[block])[:, None, None] * running + updates[block]
        leading = leading + totals[block]
    local_start = jnp.stack(start_list)
    lead_sums = jnp.stack(lead_list)
    incoming = window_scan(jnp.exp(leading), running, "ctx", 1)
    states = local_start + jnp.exp(lead_sums)[:, :, None, None] * incoming[None]
    rounded = states.astype(jnp.bfloat16)
    inter = decay_in * jnp.einsum(
        "cthe,chef->cthf", query_c, rounded, preferred_element_type=jnp.float32
    )
    attn = intra + inter
    square = jnp.mean(attn * attn, axis=-1, keepdims=True)
    inverse = lax.rsqrt(square + NORM_EPS)
    normed = attn * inverse
    silu_gate = jax.nn.silu(gate_pre.reshape(shaped).astype(jnp.float32))
    mixed = (normed * silu_gate).astype(jnp.bfloat16).reshape(tok_local, width_local)
    features = lax.all_gather(out_grad, "head", axis=2, tiled=True)[0]
    weight_b = out_weight.astype(jnp.bfloat16)
    columns = features
    mixed_grad = jnp.dot(
        columns,
        lax.all_gather(
            lax.all_gather(weight_b, "fsdp", axis=0, tiled=True), "ctx", axis=0, tiled=True
        ),
        preferred_element_type=jnp.float32,
    )
    columns = features
    grad_rows = lax.psum_scatter(
        lax.psum_scatter(
            jnp.einsum("td,th->dh", columns, mixed, preferred_element_type=jnp.float32).astype(
                jnp.bfloat16
            ),
            "ctx",
            scatter_dimension=0,
            tiled=True,
        ).astype(jnp.float32),
        "fsdp",
        scatter_dimension=0,
        tiled=True,
    )
    normed_grad = mixed_grad.reshape(shaped) * silu_gate
    inner = jnp.mean(normed_grad * normed, axis=-1, keepdims=True)
    attn_grad = (inverse * (normed_grad - normed * inner)).astype(jnp.bfloat16)
    inners = jnp.einsum("cthf,cuhf->chtu", attn_grad, value_c, preferred_element_type=jnp.float32)
    dprobs = (inners * masking).astype(jnp.bfloat16)
    qgrad = jnp.einsum("chtu,cuhe->cthe", dprobs, key_c, preferred_element_type=jnp.float32)
    kgrad = jnp.einsum("chtu,cthe->cuhe", dprobs, query_c, preferred_element_type=jnp.float32)
    vgrad = jnp.einsum("chtu,cthf->cuhf", probs, attn_grad, preferred_element_type=jnp.float32)
    weighted = (decay_in * query_c).astype(jnp.bfloat16)
    back_updates = jnp.einsum(
        "cthe,cthf->chef", weighted, attn_grad, preferred_element_type=jnp.float32
    )
    backing = jnp.zeros((head_local, HEAD_DIM, HEAD_DIM), jnp.float32)
    trailing = jnp.zeros((head_local,), jnp.float32)
    after_list = [None] * blocks
    trail_list = [None] * blocks
    for block in reversed(range(blocks)):
        after_list[block] = backing
        trail_list[block] = trailing
        backing = jnp.exp(totals[block])[:, None, None] * backing + back_updates[block]
        trailing = trailing + totals[block]
    local_after = jnp.stack(after_list)
    trail_sums = jnp.stack(trail_list)
    arriving = window_scan(jnp.exp(leading), backing, "ctx", -1)
    after_full = local_after + jnp.exp(trail_sums)[:, :, None, None] * arriving[None]
    back_b = after_full.astype(jnp.bfloat16)
    qgrad = qgrad + decay_in * jnp.einsum(
        "cthf,chef->cthe", attn_grad, rounded, preferred_element_type=jnp.float32
    )
    kgrad = kgrad + decay_out * jnp.einsum(
        "cuhf,chef->cuhe", value_c, back_b, preferred_element_type=jnp.float32
    )
    vgrad = vgrad + decay_out * jnp.einsum(
        "cuhe,chef->cuhf", key_c, back_b, preferred_element_type=jnp.float32
    )
    query_grad = qgrad.astype(jnp.bfloat16).reshape(1, tok_local, width_local)
    key_grad = kgrad.astype(jnp.bfloat16).reshape(1, tok_local, width_local)
    value_grad = vgrad.astype(jnp.bfloat16).reshape(1, tok_local, width_local)
    token_count = tok_local * lax.axis_size("ctx") * lax.axis_size("fsdp")
    grad = grad_rows / jnp.sqrt(jnp.float32(token_count))
    row_group = jnp.repeat(group_ids, ROW_BLOCK)[:, None]
    stepped = step_count[0].astype(jnp.float32)
    first = BETA_ONE * moment_one + (1.0 - BETA_ONE) * grad
    second = BETA_TWO * moment_two + (1.0 - BETA_TWO) * grad * grad
    correct_one = 1.0 - jnp.power(BETA_ONE, stepped)
    correct_two = 1.0 - jnp.power(BETA_TWO, stepped)
    active = row_group >= 1
    decayed = (row_group == 2).astype(jnp.float32)
    direction = (
        first / correct_one / (jnp.sqrt(second / correct_two) + ADAM_EPS)
        + WEIGHT_DECAY * decayed * out_weight
    )
    new_moment_one = jnp.where(active, first, moment_one)
    new_moment_two = jnp.where(active, second, moment_two)
    weight_step = jnp.where(active, direction, 0.0)
    return (query_grad, key_grad, value_grad, new_moment_one, new_moment_two, weight_step)


def solution(mesh):
    in_specs = (
        P("fsdp", "ctx", "head"),
        P("fsdp", "ctx", "head"),
        P("fsdp", "ctx", "head"),
        P("fsdp", "ctx", "head"),
        P("fsdp", "ctx", "head"),
        P("fsdp", "ctx", "head"),
        P(("ctx", "fsdp"), "head"),
        P(("ctx", "fsdp"), "head"),
        P(("ctx", "fsdp"), "head"),
        P(("ctx", "fsdp")),
        P(),
    )
    out_specs = (
        P("fsdp", "ctx", "head"),
        P("fsdp", "ctx", "head"),
        P("fsdp", "ctx", "head"),
        P(("ctx", "fsdp"), "head"),
        P(("ctx", "fsdp"), "head"),
        P(("ctx", "fsdp"), "head"),
    )
    return jax.shard_map(
        per_device, mesh=mesh, in_specs=in_specs, out_specs=out_specs, check_vma=False
    )
```

```python
import jax
import jax.numpy as jnp
from jax import lax
from jax.sharding import PartitionSpec as P

HEAD_DIM = 128
SPAN = 256
ROW_BLOCK = 32


NORM_EPS = 1e-06
BETA_ONE = 0.9
BETA_TWO = 0.95
ADAM_EPS = 1e-08
WEIGHT_DECAY = 0.1


def window_scan(gain, state, axis, sign):
    count = lax.axis_size(axis)
    place = lax.axis_index(axis)

    def join(near, far):
        return (near[0] * far[0], near[1] + near[0][:, None, None] * far[1])

    def fetch(value, step):
        high = value[0].astype(jnp.bfloat16)
        low = (value[0] - high.astype(jnp.float32)).astype(jnp.bfloat16)
        extra = jnp.broadcast_to(jnp.stack([high, low], axis=1)[:, :, None], (value[1].shape[0], 2, value[1].shape[2]))
        packed = jnp.concatenate([value[1].astype(jnp.bfloat16), extra], axis=1)
        pairs = [(i, i + sign * step) for i in range(count) if 0 <= i + sign * step < count]
        got = lax.ppermute(packed, axis, pairs).astype(jnp.float32)
        rows = value[1].shape[1]
        got = (got[:, rows, 0] + got[:, rows + 1, 0], got[:, :rows])
        source = place - sign * step
        present = (source >= 0) & (source < count)
        return jax.tree.map(lambda g, e: jnp.where(present, g, e), got, identity)

    own = (gain, state)
    identity = (jnp.ones_like(gain), jnp.zeros_like(state))
    near = [fetch(own, step) for step in (1, 2, 3)]
    inner = join(join(near[0], near[1]), near[2])
    window = join(own, inner)
    total = inner
    for step in (4, 8, 12):
        total = join(total, fetch(window, step))
    return total[1]


def decay_mask(cumul):
    along = jnp.swapaxes(cumul, 1, 2)
    spread = along[:, :, :, None] - along[:, :, None, :]
    length = cumul.shape[1]
    lower = jnp.tril(jnp.ones((length, length), jnp.float32))
    return jnp.exp(jnp.minimum(spread, 0.0)) * lower


def per_device(
    queries,
    keys,
    values,
    gate_pre,
    log_decay,
    out_grad,
    out_weight,
    moment_one,
    moment_two,
    group_ids,
    step_count,
):
    tok_local = queries.shape[1]
    head_local = log_decay.shape[2]
    width_local = queries.shape[2]
    blocks = tok_local // SPAN
    features = lax.all_gather(out_grad, "head", axis=2, tiled=True)[0]
    features, weight_b = lax.optimization_barrier((features, out_weight.astype(jnp.bfloat16)))
    shaped = (blocks, SPAN, head_local, HEAD_DIM)
    query_c = queries.reshape(shaped)
    key_c = keys.reshape(shaped)
    value_c = values.reshape(shaped)
    cumul = jnp.cumsum(log_decay.reshape(blocks, SPAN, head_local), axis=1)
    totals = cumul[:, -1, :]
    masking = decay_mask(cumul)
    decay_in = jnp.exp(cumul)[..., None]
    decay_out = jnp.exp(totals[:, None, :] - cumul)[..., None]
    scores = jnp.einsum("cthe,cuhe->chtu", query_c, key_c, preferred_element_type=jnp.float32)
    probs = (scores * masking).astype(jnp.bfloat16)
    intra = jnp.einsum("chtu,cuhe->cthe", probs, value_c, preferred_element_type=jnp.float32)
    scaled = (decay_out * key_c).astype(jnp.bfloat16)
    updates = jnp.einsum("cthe,cthf->chef", scaled, value_c, preferred_element_type=jnp.float32)
    running = jnp.zeros((head_local, HEAD_DIM, HEAD_DIM), jnp.float32)
    leading = jnp.zeros((head_local,), jnp.float32)
    start_list = []
    lead_list = []
    for block in range(blocks):
        start_list.append(running)
        lead_list.append(leading)
        running = jnp.exp(totals[block])[:, None, None] * running + updates[block]
        leading = leading + totals[block]
    local_start = jnp.stack(start_list)
    lead_sums = jnp.stack(lead_list)
    incoming = window_scan(jnp.exp(leading), running, "ctx", 1)
    states = local_start + jnp.exp(lead_sums)[:, :, None, None] * incoming[None]
    rounded = states.astype(jnp.bfloat16)
    inter = decay_in * jnp.einsum(
        "cthe,chef->cthf", query_c, rounded, preferred_element_type=jnp.float32
    )
    attn = intra + inter
    square = jnp.mean(attn * attn, axis=-1, keepdims=True)
    inverse = lax.rsqrt(square + NORM_EPS)
    normed = attn * inverse
    silu_gate = jax.nn.silu(gate_pre.reshape(shaped).astype(jnp.float32))
    mixed = (normed * silu_gate).astype(jnp.bfloat16).reshape(tok_local, width_local)
    columns = features
    mixed_grad = jnp.dot(
        columns,
        lax.all_gather(
            lax.all_gather(weight_b, "fsdp", axis=0, tiled=True), "ctx", axis=0, tiled=True
        ),
        preferred_element_type=jnp.float32,
    )
    columns = features
    grad_rows = lax.psum_scatter(
        lax.psum_scatter(
            jnp.einsum("td,th->dh", columns, mixed, preferred_element_type=jnp.float32).astype(
                jnp.bfloat16
            ),
            "ctx",
            scatter_dimension=0,
            tiled=True,
        ),
        "fsdp",
        scatter_dimension=0,
        tiled=True,
    ).astype(jnp.float32)
    normed_grad = mixed_grad.reshape(shaped) * silu_gate
    inner = jnp.mean(normed_grad * normed, axis=-1, keepdims=True)
    attn_grad = (inverse * (normed_grad - normed * inner)).astype(jnp.bfloat16)
    inners = jnp.einsum("cthf,cuhf->chtu", attn_grad, value_c, preferred_element_type=jnp.float32)
    dprobs = (inners * masking).astype(jnp.bfloat16)
    qgrad = jnp.einsum("chtu,cuhe->cthe", dprobs, key_c, preferred_element_type=jnp.float32)
    kgrad = jnp.einsum("chtu,cthe->cuhe", dprobs, query_c, preferred_element_type=jnp.float32)
    vgrad = jnp.einsum("chtu,cthf->cuhf", probs, attn_grad, preferred_element_type=jnp.float32)
    weighted = (decay_in * query_c).astype(jnp.bfloat16)
    back_updates = jnp.einsum(
        "cthe,cthf->chef", weighted, attn_grad, preferred_element_type=jnp.float32
    )
    backing = jnp.zeros((head_local, HEAD_DIM, HEAD_DIM), jnp.float32)
    trailing = jnp.zeros((head_local,), jnp.float32)
    after_list = [None] * blocks
    trail_list = [None] * blocks
    for block in reversed(range(blocks)):
        after_list[block] = backing
        trail_list[block] = trailing
        backing = jnp.exp(totals[block])[:, None, None] * backing + back_updates[block]
        trailing = trailing + totals[block]
    local_after = jnp.stack(after_list)
    trail_sums = jnp.stack(trail_list)
    arriving = window_scan(jnp.exp(leading), backing, "ctx", -1)
    after_full = local_after + jnp.exp(trail_sums)[:, :, None, None] * arriving[None]
    back_b = after_full.astype(jnp.bfloat16)
    qgrad = qgrad + decay_in * jnp.einsum(
        "cthf,chef->cthe", attn_grad, rounded, preferred_element_type=jnp.float32
    )
    kgrad = kgrad + decay_out * jnp.einsum(
        "cuhf,chef->cuhe", value_c, back_b, preferred_element_type=jnp.float32
    )
    vgrad = vgrad + decay_out * jnp.einsum(
        "cuhe,chef->cuhf", key_c, back_b, preferred_element_type=jnp.float32
    )
    query_grad = qgrad.astype(jnp.bfloat16).reshape(1, tok_local, width_local)
    key_grad = kgrad.astype(jnp.bfloat16).reshape(1, tok_local, width_local)
    value_grad = vgrad.astype(jnp.bfloat16).reshape(1, tok_local, width_local)
    token_count = tok_local * lax.axis_size("ctx") * lax.axis_size("fsdp")
    grad = grad_rows / jnp.sqrt(jnp.float32(token_count))
    row_group = jnp.repeat(group_ids, ROW_BLOCK)[:, None]
    stepped = step_count[0].astype(jnp.float32)
    first = BETA_ONE * moment_one + (1.0 - BETA_ONE) * grad
    second = BETA_TWO * moment_two + (1.0 - BETA_TWO) * grad * grad
    correct_one = 1.0 - jnp.power(BETA_ONE, stepped)
    correct_two = 1.0 - jnp.power(BETA_TWO, stepped)
    active = row_group >= 1
    decayed = (row_group == 2).astype(jnp.float32)
    direction = (
        first / correct_one / (jnp.sqrt(second / correct_two) + ADAM_EPS)
        + WEIGHT_DECAY * decayed * out_weight
    )
    new_moment_one = jnp.where(active, first, moment_one)
    new_moment_two = jnp.where(active, second, moment_two)
    weight_step = jnp.where(active, direction, 0.0)
    return (query_grad, key_grad, value_grad, new_moment_one, new_moment_two, weight_step)


def solution(mesh):
    in_specs = (
        P("fsdp", "ctx", "head"),
        P("fsdp", "ctx", "head"),
        P("fsdp", "ctx", "head"),
        P("fsdp", "ctx", "head"),
        P("fsdp", "ctx", "head"),
        P("fsdp", "ctx", "head"),
        P(("ctx", "fsdp"), "head"),
        P(("ctx", "fsdp"), "head"),
        P(("ctx", "fsdp"), "head"),
        P(("ctx", "fsdp")),
        P(),
    )
    out_specs = (
        P("fsdp", "ctx", "head"),
        P("fsdp", "ctx", "head"),
        P("fsdp", "ctx", "head"),
        P(("ctx", "fsdp"), "head"),
        P(("ctx", "fsdp"), "head"),
        P(("ctx", "fsdp"), "head"),
    )
    return jax.shard_map(
        per_device, mesh=mesh, in_specs=in_specs, out_specs=out_specs, check_vma=False
    )
```

```python
import jax
import jax.numpy as jnp
from jax import lax
from jax.sharding import PartitionSpec as P

HEAD_DIM = 128
SPAN = 256
ROW_BLOCK = 32


NORM_EPS = 1e-06
BETA_ONE = 0.9
BETA_TWO = 0.95
ADAM_EPS = 1e-08
WEIGHT_DECAY = 0.1


def window_scan(gain, state, axis, sign):
    count = lax.axis_size(axis)
    place = lax.axis_index(axis)

    def join(near, far):
        return (near[0] * far[0], near[1] + near[0][:, None, None] * far[1])

    def fetch(value, step):
        high = value[0].astype(jnp.bfloat16)
        low = (value[0] - high.astype(jnp.float32)).astype(jnp.bfloat16)
        extra = jnp.broadcast_to(jnp.stack([high, low], axis=1)[:, :, None], (value[1].shape[0], 2, value[1].shape[2]))
        packed = jnp.concatenate([value[1].astype(jnp.bfloat16), extra], axis=1)
        pairs = [(i, i + sign * step) for i in range(count) if 0 <= i + sign * step < count]
        got = lax.ppermute(packed, axis, pairs).astype(jnp.float32)
        rows = value[1].shape[1]
        got = (got[:, rows, 0] + got[:, rows + 1, 0], got[:, :rows])
        source = place - sign * step
        present = (source >= 0) & (source < count)
        return jax.tree.map(lambda g, e: jnp.where(present, g, e), got, identity)

    own = (gain, state)
    identity = (jnp.ones_like(gain), jnp.zeros_like(state))
    near = [fetch(own, step) for step in (1, 2, 3)]
    inner = join(join(near[0], near[1]), near[2])
    window = join(own, inner)
    total = inner
    for step in (4, 8, 12):
        total = join(total, fetch(window, step))
    return total[1]


def decay_mask(cumul):
    along = jnp.swapaxes(cumul, 1, 2)
    spread = along[:, :, :, None] - along[:, :, None, :]
    length = cumul.shape[1]
    lower = jnp.tril(jnp.ones((length, length), jnp.float32))
    return jnp.exp(jnp.minimum(spread, 0.0)) * lower


def per_device(
    queries,
    keys,
    values,
    gate_pre,
    log_decay,
    out_grad,
    out_weight,
    moment_one,
    moment_two,
    group_ids,
    step_count,
):
    tok_local = queries.shape[1]
    head_local = log_decay.shape[2]
    width_local = queries.shape[2]
    blocks = tok_local // SPAN
    features = lax.all_gather(out_grad, "head", axis=2, tiled=True)[0]
    weight_part = lax.all_gather(out_weight.astype(jnp.bfloat16), "fsdp", axis=0, tiled=True)
    features, weight_part = lax.optimization_barrier((features, weight_part))
    shaped = (blocks, SPAN, head_local, HEAD_DIM)
    query_c = queries.reshape(shaped)
    key_c = keys.reshape(shaped)
    value_c = values.reshape(shaped)
    cumul = jnp.cumsum(log_decay.reshape(blocks, SPAN, head_local), axis=1)
    totals = cumul[:, -1, :]
    masking = decay_mask(cumul)
    decay_in = jnp.exp(cumul)[..., None]
    decay_out = jnp.exp(totals[:, None, :] - cumul)[..., None]
    scores = jnp.einsum("cthe,cuhe->chtu", query_c, key_c, preferred_element_type=jnp.float32)
    probs = (scores * masking).astype(jnp.bfloat16)
    intra = jnp.einsum("chtu,cuhe->cthe", probs, value_c, preferred_element_type=jnp.float32)
    scaled = (decay_out * key_c).astype(jnp.bfloat16)
    updates = jnp.einsum("cthe,cthf->chef", scaled, value_c, preferred_element_type=jnp.float32)
    running = jnp.zeros((head_local, HEAD_DIM, HEAD_DIM), jnp.float32)
    leading = jnp.zeros((head_local,), jnp.float32)
    start_list = []
    lead_list = []
    for block in range(blocks):
        start_list.append(running)
        lead_list.append(leading)
        running = jnp.exp(totals[block])[:, None, None] * running + updates[block]
        leading = leading + totals[block]
    local_start = jnp.stack(start_list)
    lead_sums = jnp.stack(lead_list)
    incoming = window_scan(jnp.exp(leading), running, "ctx", 1)
    states = local_start + jnp.exp(lead_sums)[:, :, None, None] * incoming[None]
    rounded = states.astype(jnp.bfloat16)
    inter = decay_in * jnp.einsum(
        "cthe,chef->cthf", query_c, rounded, preferred_element_type=jnp.float32
    )
    attn = intra + inter
    square = jnp.mean(attn * attn, axis=-1, keepdims=True)
    inverse = lax.rsqrt(square + NORM_EPS)
    normed = attn * inverse
    silu_gate = jax.nn.silu(gate_pre.reshape(shaped).astype(jnp.float32))
    mixed = (normed * silu_gate).astype(jnp.bfloat16).reshape(tok_local, width_local)
    columns = features
    mixed_grad = jnp.dot(
        columns,
        lax.all_gather(weight_part, "ctx", axis=0, tiled=True),
        preferred_element_type=jnp.float32,
    )
    columns = features
    grad_rows = lax.psum_scatter(
        lax.psum_scatter(
            jnp.einsum("td,th->dh", columns, mixed, preferred_element_type=jnp.float32).astype(
                jnp.bfloat16
            ),
            "ctx",
            scatter_dimension=0,
            tiled=True,
        ),
        "fsdp",
        scatter_dimension=0,
        tiled=True,
    ).astype(jnp.float32)
    normed_grad = mixed_grad.reshape(shaped) * silu_gate
    inner = jnp.mean(normed_grad * normed, axis=-1, keepdims=True)
    attn_grad = (inverse * (normed_grad - normed * inner)).astype(jnp.bfloat16)
    inners = jnp.einsum("cthf,cuhf->chtu", attn_grad, value_c, preferred_element_type=jnp.float32)
    dprobs = (inners * masking).astype(jnp.bfloat16)
    qgrad = jnp.einsum("chtu,cuhe->cthe", dprobs, key_c, preferred_element_type=jnp.float32)
    kgrad = jnp.einsum("chtu,cthe->cuhe", dprobs, query_c, preferred_element_type=jnp.float32)
    vgrad = jnp.einsum("chtu,cthf->cuhf", probs, attn_grad, preferred_element_type=jnp.float32)
    weighted = (decay_in * query_c).astype(jnp.bfloat16)
    back_updates = jnp.einsum(
        "cthe,cthf->chef", weighted, attn_grad, preferred_element_type=jnp.float32
    )
    backing = jnp.zeros((head_local, HEAD_DIM, HEAD_DIM), jnp.float32)
    trailing = jnp.zeros((head_local,), jnp.float32)
    after_list = [None] * blocks
    trail_list = [None] * blocks
    for block in reversed(range(blocks)):
        after_list[block] = backing
        trail_list[block] = trailing
        backing = jnp.exp(totals[block])[:, None, None] * backing + back_updates[block]
        trailing = trailing + totals[block]
    local_after = jnp.stack(after_list)
    trail_sums = jnp.stack(trail_list)
    arriving = window_scan(jnp.exp(leading), backing, "ctx", -1)
    after_full = local_after + jnp.exp(trail_sums)[:, :, None, None] * arriving[None]
    back_b = after_full.astype(jnp.bfloat16)
    qgrad = qgrad + decay_in * jnp.einsum(
        "cthf,chef->cthe", attn_grad, rounded, preferred_element_type=jnp.float32
    )
    kgrad = kgrad + decay_out * jnp.einsum(
        "cuhf,chef->cuhe", value_c, back_b, preferred_element_type=jnp.float32
    )
    vgrad = vgrad + decay_out * jnp.einsum(
        "cuhe,chef->cuhf", key_c, back_b, preferred_element_type=jnp.float32
    )
    query_grad = qgrad.astype(jnp.bfloat16).reshape(1, tok_local, width_local)
    key_grad = kgrad.astype(jnp.bfloat16).reshape(1, tok_local, width_local)
    value_grad = vgrad.astype(jnp.bfloat16).reshape(1, tok_local, width_local)
    token_count = tok_local * lax.axis_size("ctx") * lax.axis_size("fsdp")
    grad = grad_rows / jnp.sqrt(jnp.float32(token_count))
    row_group = jnp.repeat(group_ids, ROW_BLOCK)[:, None]
    stepped = step_count[0].astype(jnp.float32)
    first = BETA_ONE * moment_one + (1.0 - BETA_ONE) * grad
    second = BETA_TWO * moment_two + (1.0 - BETA_TWO) * grad * grad
    correct_one = 1.0 - jnp.power(BETA_ONE, stepped)
    correct_two = 1.0 - jnp.power(BETA_TWO, stepped)
    active = row_group >= 1
    decayed = (row_group == 2).astype(jnp.float32)
    direction = (
        first / correct_one / (jnp.sqrt(second / correct_two) + ADAM_EPS)
        + WEIGHT_DECAY * decayed * out_weight
    )
    new_moment_one = jnp.where(active, first, moment_one)
    new_moment_two = jnp.where(active, second, moment_two)
    weight_step = jnp.where(active, direction, 0.0)
    return (query_grad, key_grad, value_grad, new_moment_one, new_moment_two, weight_step)


def solution(mesh):
    in_specs = (
        P("fsdp", "ctx", "head"),
        P("fsdp", "ctx", "head"),
        P("fsdp", "ctx", "head"),
        P("fsdp", "ctx", "head"),
        P("fsdp", "ctx", "head"),
        P("fsdp", "ctx", "head"),
        P(("ctx", "fsdp"), "head"),
        P(("ctx", "fsdp"), "head"),
        P(("ctx", "fsdp"), "head"),
        P(("ctx", "fsdp")),
        P(),
    )
    out_specs = (
        P("fsdp", "ctx", "head"),
        P("fsdp", "ctx", "head"),
        P("fsdp", "ctx", "head"),
        P(("ctx", "fsdp"), "head"),
        P(("ctx", "fsdp"), "head"),
        P(("ctx", "fsdp"), "head"),
    )
    return jax.shard_map(
        per_device, mesh=mesh, in_specs=in_specs, out_specs=out_specs, check_vma=False
    )
```

```python
import jax
import jax.numpy as jnp
from jax import lax
from jax.sharding import PartitionSpec as P

HEAD_DIM = 128
SPAN = 256
ROW_BLOCK = 32


NORM_EPS = 1e-06
BETA_ONE = 0.9
BETA_TWO = 0.95
ADAM_EPS = 1e-08
WEIGHT_DECAY = 0.1


def window_scan(gain, state, axis, sign):
    count = lax.axis_size(axis)
    place = lax.axis_index(axis)

    def join(near, far):
        return (near[0] * far[0], near[1] + near[0][:, None, None] * far[1])

    def fetch(value, step):
        high = value[0].astype(jnp.bfloat16)
        low = (value[0] - high.astype(jnp.float32)).astype(jnp.bfloat16)
        extra = jnp.broadcast_to(jnp.stack([high, low], axis=1)[:, :, None], (value[1].shape[0], 2, value[1].shape[2]))
        packed = jnp.concatenate([value[1].astype(jnp.bfloat16), extra], axis=1)
        pairs = [(i, i + sign * step) for i in range(count) if 0 <= i + sign * step < count]
        got = lax.ppermute(packed, axis, pairs).astype(jnp.float32)
        rows = value[1].shape[1]
        got = (got[:, rows, 0] + got[:, rows + 1, 0], got[:, :rows])
        source = place - sign * step
        present = (source >= 0) & (source < count)
        return jax.tree.map(lambda g, e: jnp.where(present, g, e), got, identity)

    own = (gain, state)
    identity = (jnp.ones_like(gain), jnp.zeros_like(state))
    near = [fetch(own, step) for step in (1, 2, 3)]
    inner = join(join(near[0], near[1]), near[2])
    window = join(own, inner)
    total = inner
    for step in (4, 8, 12):
        total = join(total, fetch(window, step))
    return total[1]


def decay_mask(cumul):
    along = jnp.swapaxes(cumul, 1, 2)
    spread = along[:, :, :, None] - along[:, :, None, :]
    length = cumul.shape[1]
    lower = jnp.tril(jnp.ones((length, length), jnp.float32))
    return jnp.exp(jnp.minimum(spread, 0.0)) * lower


def per_device(
    queries,
    keys,
    values,
    gate_pre,
    log_decay,
    out_grad,
    out_weight,
    moment_one,
    moment_two,
    group_ids,
    step_count,
):
    tok_local = queries.shape[1]
    head_local = log_decay.shape[2]
    width_local = queries.shape[2]
    blocks = tok_local // SPAN
    features = lax.all_gather(out_grad, "head", axis=2, tiled=True)[0]
    weight_part = lax.all_gather(out_weight.astype(jnp.bfloat16), "fsdp", axis=0, tiled=True)
    features, weight_part = lax.optimization_barrier((features, weight_part))
    shaped = (blocks, SPAN, head_local, HEAD_DIM)
    query_c = queries.reshape(shaped)
    key_c = keys.reshape(shaped)
    value_c = values.reshape(shaped)
    cumul = jnp.cumsum(log_decay.reshape(blocks, SPAN, head_local), axis=1)
    totals = cumul[:, -1, :]
    masking = decay_mask(cumul)
    decay_in = jnp.exp(cumul)[..., None]
    decay_out = jnp.exp(totals[:, None, :] - cumul)[..., None]
    scores = jnp.einsum("cthe,cuhe->chtu", query_c, key_c, preferred_element_type=jnp.float32)
    probs = (scores * masking).astype(jnp.bfloat16)
    intra = jnp.einsum("chtu,cuhe->cthe", probs, value_c, preferred_element_type=jnp.float32)
    scaled = (decay_out * key_c).astype(jnp.bfloat16)
    updates = jnp.einsum("cthe,cthf->chef", scaled, value_c, preferred_element_type=jnp.float32)
    running = jnp.zeros((head_local, HEAD_DIM, HEAD_DIM), jnp.float32)
    leading = jnp.zeros((head_local,), jnp.float32)
    start_list = []
    lead_list = []
    for block in range(blocks):
        start_list.append(running)
        lead_list.append(leading)
        running = jnp.exp(totals[block])[:, None, None] * running + updates[block]
        leading = leading + totals[block]
    local_start = jnp.stack(start_list)
    lead_sums = jnp.stack(lead_list)
    incoming = window_scan(jnp.exp(leading), running, "ctx", 1)
    states = local_start + jnp.exp(lead_sums)[:, :, None, None] * incoming[None]
    rounded = states.astype(jnp.bfloat16)
    inter = decay_in * jnp.einsum(
        "cthe,chef->cthf", query_c, rounded, preferred_element_type=jnp.float32
    )
    attn = intra + inter
    square = jnp.mean(attn * attn, axis=-1, keepdims=True)
    inverse = lax.rsqrt(square + NORM_EPS)
    normed = attn * inverse
    silu_gate = jax.nn.silu(gate_pre.reshape(shaped).astype(jnp.float32))
    mixed = (normed * silu_gate).astype(jnp.bfloat16).reshape(tok_local, width_local)
    columns = features
    partial = jnp.einsum("td,th->dh", columns, mixed, preferred_element_type=jnp.float32).astype(
        jnp.bfloat16
    )
    weight_full, partial = lax.optimization_barrier(
        (lax.all_gather(weight_part, "ctx", axis=0, tiled=True), partial)
    )
    mixed_grad = jnp.dot(columns, weight_full, preferred_element_type=jnp.float32)
    grad_rows = lax.psum_scatter(
        lax.psum_scatter(partial, "ctx", scatter_dimension=0, tiled=True),
        "fsdp",
        scatter_dimension=0,
        tiled=True,
    ).astype(jnp.float32)
    normed_grad = mixed_grad.reshape(shaped) * silu_gate
    inner = jnp.mean(normed_grad * normed, axis=-1, keepdims=True)
    attn_grad = (inverse * (normed_grad - normed * inner)).astype(jnp.bfloat16)
    inners = jnp.einsum("cthf,cuhf->chtu", attn_grad, value_c, preferred_element_type=jnp.float32)
    dprobs = (inners * masking).astype(jnp.bfloat16)
    qgrad = jnp.einsum("chtu,cuhe->cthe", dprobs, key_c, preferred_element_type=jnp.float32)
    kgrad = jnp.einsum("chtu,cthe->cuhe", dprobs, query_c, preferred_element_type=jnp.float32)
    vgrad = jnp.einsum("chtu,cthf->cuhf", probs, attn_grad, preferred_element_type=jnp.float32)
    weighted = (decay_in * query_c).astype(jnp.bfloat16)
    back_updates = jnp.einsum(
        "cthe,cthf->chef", weighted, attn_grad, preferred_element_type=jnp.float32
    )
    backing = jnp.zeros((head_local, HEAD_DIM, HEAD_DIM), jnp.float32)
    trailing = jnp.zeros((head_local,), jnp.float32)
    after_list = [None] * blocks
    trail_list = [None] * blocks
    for block in reversed(range(blocks)):
        after_list[block] = backing
        trail_list[block] = trailing
        backing = jnp.exp(totals[block])[:, None, None] * backing + back_updates[block]
        trailing = trailing + totals[block]
    local_after = jnp.stack(after_list)
    trail_sums = jnp.stack(trail_list)
    arriving = window_scan(jnp.exp(leading), backing, "ctx", -1)
    after_full = local_after + jnp.exp(trail_sums)[:, :, None, None] * arriving[None]
    back_b = after_full.astype(jnp.bfloat16)
    qgrad = qgrad + decay_in * jnp.einsum(
        "cthf,chef->cthe", attn_grad, rounded, preferred_element_type=jnp.float32
    )
    kgrad = kgrad + decay_out * jnp.einsum(
        "cuhf,chef->cuhe", value_c, back_b, preferred_element_type=jnp.float32
    )
    vgrad = vgrad + decay_out * jnp.einsum(
        "cuhe,chef->cuhf", key_c, back_b, preferred_element_type=jnp.float32
    )
    query_grad = qgrad.astype(jnp.bfloat16).reshape(1, tok_local, width_local)
    key_grad = kgrad.astype(jnp.bfloat16).reshape(1, tok_local, width_local)
    value_grad = vgrad.astype(jnp.bfloat16).reshape(1, tok_local, width_local)
    token_count = tok_local * lax.axis_size("ctx") * lax.axis_size("fsdp")
    grad = grad_rows / jnp.sqrt(jnp.float32(token_count))
    row_group = jnp.repeat(group_ids, ROW_BLOCK)[:, None]
    stepped = step_count[0].astype(jnp.float32)
    first = BETA_ONE * moment_one + (1.0 - BETA_ONE) * grad
    second = BETA_TWO * moment_two + (1.0 - BETA_TWO) * grad * grad
    correct_one = 1.0 - jnp.power(BETA_ONE, stepped)
    correct_two = 1.0 - jnp.power(BETA_TWO, stepped)
    active = row_group >= 1
    decayed = (row_group == 2).astype(jnp.float32)
    direction = (
        first / correct_one / (jnp.sqrt(second / correct_two) + ADAM_EPS)
        + WEIGHT_DECAY * decayed * out_weight
    )
    new_moment_one = jnp.where(active, first, moment_one)
    new_moment_two = jnp.where(active, second, moment_two)
    weight_step = jnp.where(active, direction, 0.0)
    return (query_grad, key_grad, value_grad, new_moment_one, new_moment_two, weight_step)


def solution(mesh):
    in_specs = (
        P("fsdp", "ctx", "head"),
        P("fsdp", "ctx", "head"),
        P("fsdp", "ctx", "head"),
        P("fsdp", "ctx", "head"),
        P("fsdp", "ctx", "head"),
        P("fsdp", "ctx", "head"),
        P(("ctx", "fsdp"), "head"),
        P(("ctx", "fsdp"), "head"),
        P(("ctx", "fsdp"), "head"),
        P(("ctx", "fsdp")),
        P(),
    )
    out_specs = (
        P("fsdp", "ctx", "head"),
        P("fsdp", "ctx", "head"),
        P("fsdp", "ctx", "head"),
        P(("ctx", "fsdp"), "head"),
        P(("ctx", "fsdp"), "head"),
        P(("ctx", "fsdp"), "head"),
    )
    return jax.shard_map(
        per_device, mesh=mesh, in_specs=in_specs, out_specs=out_specs, check_vma=False
    )
```

```python
import jax
import jax.numpy as jnp
from jax import lax
from jax.sharding import PartitionSpec as P

HEAD_DIM = 128
SPAN = 256
ROW_BLOCK = 32


NORM_EPS = 1e-06
BETA_ONE = 0.9
BETA_TWO = 0.95
ADAM_EPS = 1e-08
WEIGHT_DECAY = 0.1


def window_scan(gain, state, axis, sign):
    count = lax.axis_size(axis)
    place = lax.axis_index(axis)

    def join(near, far):
        return (near[0] * far[0], near[1] + near[0][:, None, None] * far[1])

    def fetch(value, step):
        high = value[0].astype(jnp.bfloat16)
        low = (value[0] - high.astype(jnp.float32)).astype(jnp.bfloat16)
        extra = jnp.broadcast_to(jnp.stack([high, low], axis=1)[:, :, None], (value[1].shape[0], 2, value[1].shape[2]))
        packed = jnp.concatenate([value[1].astype(jnp.bfloat16), extra], axis=1)
        pairs = [(i, i + sign * step) for i in range(count) if 0 <= i + sign * step < count]
        got = lax.ppermute(packed, axis, pairs).astype(jnp.float32)
        rows = value[1].shape[1]
        got = (got[:, rows, 0] + got[:, rows + 1, 0], got[:, :rows])
        source = place - sign * step
        present = (source >= 0) & (source < count)
        return jax.tree.map(lambda g, e: jnp.where(present, g, e), got, identity)

    own = (gain, state)
    identity = (jnp.ones_like(gain), jnp.zeros_like(state))
    near = [fetch(own, step) for step in (1, 2, 3)]
    inner = join(join(near[0], near[1]), near[2])
    window = join(own, inner)
    total = inner
    for step in (4, 8, 12):
        total = join(total, fetch(window, step))
    return total[1]


def gather_features(part, axis):
    count = lax.axis_size(axis)
    if count != 4:
        whole = lax.all_gather(part, axis)
        return whole
    place = lax.axis_index(axis)
    far = lax.ppermute(part, axis, [(i, i ^ 2) for i in range(count)])
    pair = jnp.stack([part, far])
    near = lax.ppermute(pair, axis, [(i, i ^ 1) for i in range(count)])
    stacked = jnp.concatenate([pair[:1], near[:1], pair[1:], near[1:]])
    return stacked[jnp.arange(count) ^ place]


def decay_mask(cumul):
    along = jnp.swapaxes(cumul, 1, 2)
    spread = along[:, :, :, None] - along[:, :, None, :]
    length = cumul.shape[1]
    lower = jnp.tril(jnp.ones((length, length), jnp.float32))
    return jnp.exp(jnp.minimum(spread, 0.0)) * lower


def per_device(
    queries,
    keys,
    values,
    gate_pre,
    log_decay,
    out_grad,
    out_weight,
    moment_one,
    moment_two,
    group_ids,
    step_count,
):
    tok_local = queries.shape[1]
    head_local = log_decay.shape[2]
    width_local = queries.shape[2]
    blocks = tok_local // SPAN
    features = gather_features(out_grad[0], "head")
    weight_part = lax.all_gather(out_weight.astype(jnp.bfloat16), "fsdp", axis=0, tiled=True)
    shaped = (blocks, SPAN, head_local, HEAD_DIM)
    query_c = queries.reshape(shaped)
    key_c = keys.reshape(shaped)
    value_c = values.reshape(shaped)
    cumul = jnp.cumsum(log_decay.reshape(blocks, SPAN, head_local), axis=1)
    totals = cumul[:, -1, :]
    masking = decay_mask(cumul)
    decay_in = jnp.exp(cumul)[..., None]
    decay_out = jnp.exp(totals[:, None, :] - cumul)[..., None]
    scores = jnp.einsum("cthe,cuhe->chtu", query_c, key_c, preferred_element_type=jnp.float32)
    probs = (scores * masking).astype(jnp.bfloat16)
    intra = jnp.einsum("chtu,cuhe->cthe", probs, value_c, preferred_element_type=jnp.float32)
    scaled = (decay_out * key_c).astype(jnp.bfloat16)
    updates = jnp.einsum("cthe,cthf->chef", scaled, value_c, preferred_element_type=jnp.float32)
    running = jnp.zeros((head_local, HEAD_DIM, HEAD_DIM), jnp.float32)
    leading = jnp.zeros((head_local,), jnp.float32)
    start_list = []
    lead_list = []
    for block in range(blocks):
        start_list.append(running)
        lead_list.append(leading)
        running = jnp.exp(totals[block])[:, None, None] * running + updates[block]
        leading = leading + totals[block]
    local_start = jnp.stack(start_list)
    lead_sums = jnp.stack(lead_list)
    incoming = window_scan(jnp.exp(leading), running, "ctx", 1)
    states = local_start + jnp.exp(lead_sums)[:, :, None, None] * incoming[None]
    rounded = states.astype(jnp.bfloat16)
    inter = decay_in * jnp.einsum(
        "cthe,chef->cthf", query_c, rounded, preferred_element_type=jnp.float32
    )
    attn = intra + inter
    square = jnp.mean(attn * attn, axis=-1, keepdims=True)
    inverse = lax.rsqrt(square + NORM_EPS)
    normed = attn * inverse
    silu_gate = jax.nn.silu(gate_pre.reshape(shaped).astype(jnp.float32))
    mixed = (normed * silu_gate).astype(jnp.bfloat16).reshape(tok_local, width_local)
    columns = features
    partial = jnp.einsum("ktd,th->kdh", columns, mixed, preferred_element_type=jnp.float32)
    partial = partial.reshape(-1, partial.shape[2]).astype(jnp.bfloat16)
    weight_full, partial = lax.optimization_barrier(
        (lax.all_gather(weight_part, "ctx", axis=0, tiled=True), partial)
    )
    mixed_grad = jnp.einsum(
        "ktd,kdh->th",
        columns,
        weight_full.reshape(columns.shape[0], columns.shape[2], -1),
        preferred_element_type=jnp.float32,
    )
    grad_rows = lax.psum_scatter(
        lax.psum_scatter(partial, "ctx", scatter_dimension=0, tiled=True),
        "fsdp",
        scatter_dimension=0,
        tiled=True,
    ).astype(jnp.float32)
    normed_grad = mixed_grad.reshape(shaped) * silu_gate
    inner = jnp.mean(normed_grad * normed, axis=-1, keepdims=True)
    attn_grad = (inverse * (normed_grad - normed * inner)).astype(jnp.bfloat16)
    inners = jnp.einsum("cthf,cuhf->chtu", attn_grad, value_c, preferred_element_type=jnp.float32)
    dprobs = (inners * masking).astype(jnp.bfloat16)
    qgrad = jnp.einsum("chtu,cuhe->cthe", dprobs, key_c, preferred_element_type=jnp.float32)
    kgrad = jnp.einsum("chtu,cthe->cuhe", dprobs, query_c, preferred_element_type=jnp.float32)
    vgrad = jnp.einsum("chtu,cthf->cuhf", probs, attn_grad, preferred_element_type=jnp.float32)
    weighted = (decay_in * query_c).astype(jnp.bfloat16)
    back_updates = jnp.einsum(
        "cthe,cthf->chef", weighted, attn_grad, preferred_element_type=jnp.float32
    )
    backing = jnp.zeros((head_local, HEAD_DIM, HEAD_DIM), jnp.float32)
    trailing = jnp.zeros((head_local,), jnp.float32)
    after_list = [None] * blocks
    trail_list = [None] * blocks
    for block in reversed(range(blocks)):
        after_list[block] = backing
        trail_list[block] = trailing
        backing = jnp.exp(totals[block])[:, None, None] * backing + back_updates[block]
        trailing = trailing + totals[block]
    local_after = jnp.stack(after_list)
    trail_sums = jnp.stack(trail_list)
    arriving = window_scan(jnp.exp(leading), backing, "ctx", -1)
    after_full = local_after + jnp.exp(trail_sums)[:, :, None, None] * arriving[None]
    back_b = after_full.astype(jnp.bfloat16)
    qgrad = qgrad + decay_in * jnp.einsum(
        "cthf,chef->cthe", attn_grad, rounded, preferred_element_type=jnp.float32
    )
    kgrad = kgrad + decay_out * jnp.einsum(
        "cuhf,chef->cuhe", value_c, back_b, preferred_element_type=jnp.float32
    )
    vgrad = vgrad + decay_out * jnp.einsum(
        "cuhe,chef->cuhf", key_c, back_b, preferred_element_type=jnp.float32
    )
    query_grad = qgrad.astype(jnp.bfloat16).reshape(1, tok_local, width_local)
    key_grad = kgrad.astype(jnp.bfloat16).reshape(1, tok_local, width_local)
    value_grad = vgrad.astype(jnp.bfloat16).reshape(1, tok_local, width_local)
    token_count = tok_local * lax.axis_size("ctx") * lax.axis_size("fsdp")
    grad = grad_rows / jnp.sqrt(jnp.float32(token_count))
    row_group = jnp.repeat(group_ids, ROW_BLOCK)[:, None]
    stepped = step_count[0].astype(jnp.float32)
    first = BETA_ONE * moment_one + (1.0 - BETA_ONE) * grad
    second = BETA_TWO * moment_two + (1.0 - BETA_TWO) * grad * grad
    correct_one = 1.0 - jnp.power(BETA_ONE, stepped)
    correct_two = 1.0 - jnp.power(BETA_TWO, stepped)
    active = row_group >= 1
    decayed = (row_group == 2).astype(jnp.float32)
    direction = (
        first / correct_one / (jnp.sqrt(second / correct_two) + ADAM_EPS)
        + WEIGHT_DECAY * decayed * out_weight
    )
    new_moment_one = jnp.where(active, first, moment_one)
    new_moment_two = jnp.where(active, second, moment_two)
    weight_step = jnp.where(active, direction, 0.0)
    return (query_grad, key_grad, value_grad, new_moment_one, new_moment_two, weight_step)


def solution(mesh):
    in_specs = (
        P("fsdp", "ctx", "head"),
        P("fsdp", "ctx", "head"),
        P("fsdp", "ctx", "head"),
        P("fsdp", "ctx", "head"),
        P("fsdp", "ctx", "head"),
        P("fsdp", "ctx", "head"),
        P(("ctx", "fsdp"), "head"),
        P(("ctx", "fsdp"), "head"),
        P(("ctx", "fsdp"), "head"),
        P(("ctx", "fsdp")),
        P(),
    )
    out_specs = (
        P("fsdp", "ctx", "head"),
        P("fsdp", "ctx", "head"),
        P("fsdp", "ctx", "head"),
        P(("ctx", "fsdp"), "head"),
        P(("ctx", "fsdp"), "head"),
        P(("ctx", "fsdp"), "head"),
    )
    return jax.shard_map(
        per_device, mesh=mesh, in_specs=in_specs, out_specs=out_specs, check_vma=False
    )
```

```python
import jax
import jax.numpy as jnp
from jax import lax
from jax.sharding import PartitionSpec as P

HEAD_DIM = 128
SPAN = 256
ROW_BLOCK = 32


NORM_EPS = 1e-06
BETA_ONE = 0.9
BETA_TWO = 0.95
ADAM_EPS = 1e-08
WEIGHT_DECAY = 0.1


def window_scan(gain, state, axis, sign):
    count = lax.axis_size(axis)
    place = lax.axis_index(axis)

    def join(near, far):
        return (near[0] * far[0], near[1] + near[0][:, None, None] * far[1])

    def fetch(value, step):
        high = value[0].astype(jnp.bfloat16)
        low = (value[0] - high.astype(jnp.float32)).astype(jnp.bfloat16)
        extra = jnp.broadcast_to(jnp.stack([high, low], axis=1)[:, :, None], (value[1].shape[0], 2, value[1].shape[2]))
        packed = jnp.concatenate([value[1].astype(jnp.bfloat16), extra], axis=1)
        pairs = [(i, i + sign * step) for i in range(count) if 0 <= i + sign * step < count]
        got = lax.ppermute(packed, axis, pairs).astype(jnp.float32)
        rows = value[1].shape[1]
        got = (got[:, rows, 0] + got[:, rows + 1, 0], got[:, :rows])
        source = place - sign * step
        present = (source >= 0) & (source < count)
        return jax.tree.map(lambda g, e: jnp.where(present, g, e), got, identity)

    own = (gain, state)
    identity = (jnp.ones_like(gain), jnp.zeros_like(state))
    near = [fetch(own, step) for step in (1, 2, 3)]
    inner = join(join(near[0], near[1]), near[2])
    window = join(own, inner)
    total = inner
    for step in (4, 8, 12):
        total = join(total, fetch(window, step))
    return total[1]


def decay_mask(cumul):
    along = jnp.swapaxes(cumul, 1, 2)
    spread = along[:, :, :, None] - along[:, :, None, :]
    length = cumul.shape[1]
    lower = jnp.tril(jnp.ones((length, length), jnp.float32))
    return jnp.exp(jnp.minimum(spread, 0.0)) * lower


def per_device(
    queries,
    keys,
    values,
    gate_pre,
    log_decay,
    out_grad,
    out_weight,
    moment_one,
    moment_two,
    group_ids,
    step_count,
):
    tok_local = queries.shape[1]
    head_local = log_decay.shape[2]
    width_local = queries.shape[2]
    blocks = tok_local // SPAN
    features = lax.all_gather(out_grad, "head", axis=2, tiled=True)[0]
    weight_part = lax.all_gather(out_weight.astype(jnp.bfloat16), "fsdp", axis=0, tiled=True)
    features, weight_part = lax.optimization_barrier((features, weight_part))
    shaped = (blocks, SPAN, head_local, HEAD_DIM)
    query_c = queries.reshape(shaped)
    key_c = keys.reshape(shaped)
    value_c = values.reshape(shaped)
    cumul = jnp.cumsum(log_decay.reshape(blocks, SPAN, head_local), axis=1)
    totals = cumul[:, -1, :]
    masking = decay_mask(cumul)
    decay_in = jnp.exp(cumul)[..., None]
    decay_out = jnp.exp(totals[:, None, :] - cumul)[..., None]
    scores = jnp.einsum("cthe,cuhe->chtu", query_c, key_c, preferred_element_type=jnp.float32)
    probs = (scores * masking).astype(jnp.bfloat16)
    intra = jnp.einsum("chtu,cuhe->cthe", probs, value_c, preferred_element_type=jnp.float32)
    scaled = (decay_out * key_c).astype(jnp.bfloat16)
    updates = jnp.einsum("cthe,cthf->chef", scaled, value_c, preferred_element_type=jnp.float32)
    running = jnp.zeros((head_local, HEAD_DIM, HEAD_DIM), jnp.float32)
    leading = jnp.zeros((head_local,), jnp.float32)
    start_list = []
    lead_list = []
    for block in range(blocks):
        start_list.append(running)
        lead_list.append(leading)
        running = jnp.exp(totals[block])[:, None, None] * running + updates[block]
        leading = leading + totals[block]
    local_start = jnp.stack(start_list)
    lead_sums = jnp.stack(lead_list)
    incoming = window_scan(jnp.exp(leading), running, "ctx", 1)
    states = local_start + jnp.exp(lead_sums)[:, :, None, None] * incoming[None]
    rounded = states.astype(jnp.bfloat16)
    inter = decay_in * jnp.einsum(
        "cthe,chef->cthf", query_c, rounded, preferred_element_type=jnp.float32
    )
    attn = intra + inter
    square = jnp.mean(attn * attn, axis=-1, keepdims=True)
    inverse = lax.rsqrt(square + NORM_EPS)
    normed = attn * inverse
    silu_gate = jax.nn.silu(gate_pre.reshape(shaped).astype(jnp.float32))
    mixed = (normed * silu_gate).astype(jnp.bfloat16).reshape(tok_local, width_local)
    columns = features
    partial = jnp.einsum("td,th->dh", columns, mixed, preferred_element_type=jnp.float32).astype(
        jnp.bfloat16
    )
    weight_full, partial = lax.optimization_barrier(
        (lax.all_gather(weight_part, "ctx", axis=0, tiled=True), partial)
    )
    mixed_grad = jnp.dot(columns, weight_full, preferred_element_type=jnp.float32)
    by_ctx = lax.psum_scatter(partial, "ctx", scatter_dimension=0, tiled=True)
    spread = lax.axis_size("fsdp")
    grad_rows = lax.all_to_all(
        by_ctx.reshape(spread, -1, by_ctx.shape[1]), "fsdp", 0, 0, tiled=False
    ).astype(jnp.float32).sum(0)
    normed_grad = mixed_grad.reshape(shaped) * silu_gate
    inner = jnp.mean(normed_grad * normed, axis=-1, keepdims=True)
    attn_grad = (inverse * (normed_grad - normed * inner)).astype(jnp.bfloat16)
    inners = jnp.einsum("cthf,cuhf->chtu", attn_grad, value_c, preferred_element_type=jnp.float32)
    dprobs = (inners * masking).astype(jnp.bfloat16)
    qgrad = jnp.einsum("chtu,cuhe->cthe", dprobs, key_c, preferred_element_type=jnp.float32)
    kgrad = jnp.einsum("chtu,cthe->cuhe", dprobs, query_c, preferred_element_type=jnp.float32)
    vgrad = jnp.einsum("chtu,cthf->cuhf", probs, attn_grad, preferred_element_type=jnp.float32)
    weighted = (decay_in * query_c).astype(jnp.bfloat16)
    back_updates = jnp.einsum(
        "cthe,cthf->chef", weighted, attn_grad, preferred_element_type=jnp.float32
    )
    backing = jnp.zeros((head_local, HEAD_DIM, HEAD_DIM), jnp.float32)
    trailing = jnp.zeros((head_local,), jnp.float32)
    after_list = [None] * blocks
    trail_list = [None] * blocks
    for block in reversed(range(blocks)):
        after_list[block] = backing
        trail_list[block] = trailing
        backing = jnp.exp(totals[block])[:, None, None] * backing + back_updates[block]
        trailing = trailing + totals[block]
    local_after = jnp.stack(after_list)
    trail_sums = jnp.stack(trail_list)
    arriving = window_scan(jnp.exp(leading), backing, "ctx", -1)
    after_full = local_after + jnp.exp(trail_sums)[:, :, None, None] * arriving[None]
    back_b = after_full.astype(jnp.bfloat16)
    qgrad = qgrad + decay_in * jnp.einsum(
        "cthf,chef->cthe", attn_grad, rounded, preferred_element_type=jnp.float32
    )
    kgrad = kgrad + decay_out * jnp.einsum(
        "cuhf,chef->cuhe", value_c, back_b, preferred_element_type=jnp.float32
    )
    vgrad = vgrad + decay_out * jnp.einsum(
        "cuhe,chef->cuhf", key_c, back_b, preferred_element_type=jnp.float32
    )
    query_grad = qgrad.astype(jnp.bfloat16).reshape(1, tok_local, width_local)
    key_grad = kgrad.astype(jnp.bfloat16).reshape(1, tok_local, width_local)
    value_grad = vgrad.astype(jnp.bfloat16).reshape(1, tok_local, width_local)
    token_count = tok_local * lax.axis_size("ctx") * lax.axis_size("fsdp")
    grad = grad_rows / jnp.sqrt(jnp.float32(token_count))
    row_group = jnp.repeat(group_ids, ROW_BLOCK)[:, None]
    stepped = step_count[0].astype(jnp.float32)
    first = BETA_ONE * moment_one + (1.0 - BETA_ONE) * grad
    second = BETA_TWO * moment_two + (1.0 - BETA_TWO) * grad * grad
    correct_one = 1.0 - jnp.power(BETA_ONE, stepped)
    correct_two = 1.0 - jnp.power(BETA_TWO, stepped)
    active = row_group >= 1
    decayed = (row_group == 2).astype(jnp.float32)
    direction = (
        first / correct_one / (jnp.sqrt(second / correct_two) + ADAM_EPS)
        + WEIGHT_DECAY * decayed * out_weight
    )
    new_moment_one = jnp.where(active, first, moment_one)
    new_moment_two = jnp.where(active, second, moment_two)
    weight_step = jnp.where(active, direction, 0.0)
    return (query_grad, key_grad, value_grad, new_moment_one, new_moment_two, weight_step)


def solution(mesh):
    in_specs = (
        P("fsdp", "ctx", "head"),
        P("fsdp", "ctx", "head"),
        P("fsdp", "ctx", "head"),
        P("fsdp", "ctx", "head"),
        P("fsdp", "ctx", "head"),
        P("fsdp", "ctx", "head"),
        P(("ctx", "fsdp"), "head"),
        P(("ctx", "fsdp"), "head"),
        P(("ctx", "fsdp"), "head"),
        P(("ctx", "fsdp")),
        P(),
    )
    out_specs = (
        P("fsdp", "ctx", "head"),
        P("fsdp", "ctx", "head"),
        P("fsdp", "ctx", "head"),
        P(("ctx", "fsdp"), "head"),
        P(("ctx", "fsdp"), "head"),
        P(("ctx", "fsdp"), "head"),
    )
    return jax.shard_map(
        per_device, mesh=mesh, in_specs=in_specs, out_specs=out_specs, check_vma=False
    )
```

```python
import jax
import jax.numpy as jnp
from jax import lax
from jax.sharding import PartitionSpec as P

HEAD_DIM = 128
SPAN = 256
ROW_BLOCK = 32


NORM_EPS = 1e-06
BETA_ONE = 0.9
BETA_TWO = 0.95
ADAM_EPS = 1e-08
WEIGHT_DECAY = 0.1


def window_scan(gain, state, axis, sign):
    count = lax.axis_size(axis)
    place = lax.axis_index(axis)

    def join(near, far):
        return (near[0] * far[0], near[1] + near[0][:, None, None] * far[1])

    def fetch(value, step):
        high = value[0].astype(jnp.bfloat16)
        low = (value[0] - high.astype(jnp.float32)).astype(jnp.bfloat16)
        extra = jnp.broadcast_to(jnp.stack([high, low], axis=1)[:, :, None], (value[1].shape[0], 2, value[1].shape[2]))
        packed = jnp.concatenate([value[1].astype(jnp.bfloat16), extra], axis=1)
        pairs = [(i, i + sign * step) for i in range(count) if 0 <= i + sign * step < count]
        got = lax.ppermute(packed, axis, pairs).astype(jnp.float32)
        rows = value[1].shape[1]
        got = (got[:, rows, 0] + got[:, rows + 1, 0], got[:, :rows])
        source = place - sign * step
        present = (source >= 0) & (source < count)
        return jax.tree.map(lambda g, e: jnp.where(present, g, e), got, identity)

    own = (gain, state)
    identity = (jnp.ones_like(gain), jnp.zeros_like(state))
    total = fetch(own, 1)
    step = 1
    while step < count:
        total = join(total, fetch(total, step))
        step *= 2
    return total[1]


def decay_mask(cumul):
    along = jnp.swapaxes(cumul, 1, 2)
    spread = along[:, :, :, None] - along[:, :, None, :]
    length = cumul.shape[1]
    lower = jnp.tril(jnp.ones((length, length), jnp.float32))
    return jnp.exp(jnp.minimum(spread, 0.0)) * lower


def per_device(
    queries,
    keys,
    values,
    gate_pre,
    log_decay,
    out_grad,
    out_weight,
    moment_one,
    moment_two,
    group_ids,
    step_count,
):
    tok_local = queries.shape[1]
    head_local = log_decay.shape[2]
    width_local = queries.shape[2]
    blocks = tok_local // SPAN
    features = lax.all_gather(out_grad, "head", axis=2, tiled=True)[0]
    weight_part = lax.all_gather(out_weight.astype(jnp.bfloat16), "fsdp", axis=0, tiled=True)
    features, weight_part = lax.optimization_barrier((features, weight_part))
    shaped = (blocks, SPAN, head_local, HEAD_DIM)
    query_c = queries.reshape(shaped)
    key_c = keys.reshape(shaped)
    value_c = values.reshape(shaped)
    cumul = jnp.cumsum(log_decay.reshape(blocks, SPAN, head_local), axis=1)
    totals = cumul[:, -1, :]
    masking = decay_mask(cumul)
    decay_in = jnp.exp(cumul)[..., None]
    decay_out = jnp.exp(totals[:, None, :] - cumul)[..., None]
    scores = jnp.einsum("cthe,cuhe->chtu", query_c, key_c, preferred_element_type=jnp.float32)
    probs = (scores * masking).astype(jnp.bfloat16)
    intra = jnp.einsum("chtu,cuhe->cthe", probs, value_c, preferred_element_type=jnp.float32)
    scaled = (decay_out * key_c).astype(jnp.bfloat16)
    updates = jnp.einsum("cthe,cthf->chef", scaled, value_c, preferred_element_type=jnp.float32)
    running = jnp.zeros((head_local, HEAD_DIM, HEAD_DIM), jnp.float32)
    leading = jnp.zeros((head_local,), jnp.float32)
    start_list = []
    lead_list = []
    for block in range(blocks):
        start_list.append(running)
        lead_list.append(leading)
        running = jnp.exp(totals[block])[:, None, None] * running + updates[block]
        leading = leading + totals[block]
    local_start = jnp.stack(start_list)
    lead_sums = jnp.stack(lead_list)
    incoming = window_scan(jnp.exp(leading), running, "ctx", 1)
    states = local_start + jnp.exp(lead_sums)[:, :, None, None] * incoming[None]
    rounded = states.astype(jnp.bfloat16)
    inter = decay_in * jnp.einsum(
        "cthe,chef->cthf", query_c, rounded, preferred_element_type=jnp.float32
    )
    attn = intra + inter
    square = jnp.mean(attn * attn, axis=-1, keepdims=True)
    inverse = lax.rsqrt(square + NORM_EPS)
    normed = attn * inverse
    silu_gate = jax.nn.silu(gate_pre.reshape(shaped).astype(jnp.float32))
    mixed = (normed * silu_gate).astype(jnp.bfloat16).reshape(tok_local, width_local)
    columns = features
    partial = jnp.einsum("td,th->dh", columns, mixed, preferred_element_type=jnp.float32).astype(
        jnp.bfloat16
    )
    weight_full, partial = lax.optimization_barrier(
        (lax.all_gather(weight_part, "ctx", axis=0, tiled=True), partial)
    )
    mixed_grad = jnp.dot(columns, weight_full, preferred_element_type=jnp.float32)
    by_ctx = lax.psum_scatter(partial, "ctx", scatter_dimension=0, tiled=True)
    spread = lax.axis_size("fsdp")
    grad_rows = lax.all_to_all(
        by_ctx.reshape(spread, -1, by_ctx.shape[1]), "fsdp", 0, 0, tiled=False
    ).astype(jnp.float32).sum(0)
    normed_grad = mixed_grad.reshape(shaped) * silu_gate
    inner = jnp.mean(normed_grad * normed, axis=-1, keepdims=True)
    attn_grad = (inverse * (normed_grad - normed * inner)).astype(jnp.bfloat16)
    inners = jnp.einsum("cthf,cuhf->chtu", attn_grad, value_c, preferred_element_type=jnp.float32)
    dprobs = (inners * masking).astype(jnp.bfloat16)
    qgrad = jnp.einsum("chtu,cuhe->cthe", dprobs, key_c, preferred_element_type=jnp.float32)
    kgrad = jnp.einsum("chtu,cthe->cuhe", dprobs, query_c, preferred_element_type=jnp.float32)
    vgrad = jnp.einsum("chtu,cthf->cuhf", probs, attn_grad, preferred_element_type=jnp.float32)
    weighted = (decay_in * query_c).astype(jnp.bfloat16)
    back_updates = jnp.einsum(
        "cthe,cthf->chef", weighted, attn_grad, preferred_element_type=jnp.float32
    )
    backing = jnp.zeros((head_local, HEAD_DIM, HEAD_DIM), jnp.float32)
    trailing = jnp.zeros((head_local,), jnp.float32)
    after_list = [None] * blocks
    trail_list = [None] * blocks
    for block in reversed(range(blocks)):
        after_list[block] = backing
        trail_list[block] = trailing
        backing = jnp.exp(totals[block])[:, None, None] * backing + back_updates[block]
        trailing = trailing + totals[block]
    local_after = jnp.stack(after_list)
    trail_sums = jnp.stack(trail_list)
    arriving = window_scan(jnp.exp(leading), backing, "ctx", -1)
    after_full = local_after + jnp.exp(trail_sums)[:, :, None, None] * arriving[None]
    back_b = after_full.astype(jnp.bfloat16)
    qgrad = qgrad + decay_in * jnp.einsum(
        "cthf,chef->cthe", attn_grad, rounded, preferred_element_type=jnp.float32
    )
    kgrad = kgrad + decay_out * jnp.einsum(
        "cuhf,chef->cuhe", value_c, back_b, preferred_element_type=jnp.float32
    )
    vgrad = vgrad + decay_out * jnp.einsum(
        "cuhe,chef->cuhf", key_c, back_b, preferred_element_type=jnp.float32
    )
    query_grad = qgrad.astype(jnp.bfloat16).reshape(1, tok_local, width_local)
    key_grad = kgrad.astype(jnp.bfloat16).reshape(1, tok_local, width_local)
    value_grad = vgrad.astype(jnp.bfloat16).reshape(1, tok_local, width_local)
    token_count = tok_local * lax.axis_size("ctx") * lax.axis_size("fsdp")
    grad = grad_rows / jnp.sqrt(jnp.float32(token_count))
    row_group = jnp.repeat(group_ids, ROW_BLOCK)[:, None]
    stepped = step_count[0].astype(jnp.float32)
    first = BETA_ONE * moment_one + (1.0 - BETA_ONE) * grad
    second = BETA_TWO * moment_two + (1.0 - BETA_TWO) * grad * grad
    correct_one = 1.0 - jnp.power(BETA_ONE, stepped)
    correct_two = 1.0 - jnp.power(BETA_TWO, stepped)
    active = row_group >= 1
    decayed = (row_group == 2).astype(jnp.float32)
    direction = (
        first / correct_one / (jnp.sqrt(second / correct_two) + ADAM_EPS)
        + WEIGHT_DECAY * decayed * out_weight
    )
    new_moment_one = jnp.where(active, first, moment_one)
    new_moment_two = jnp.where(active, second, moment_two)
    weight_step = jnp.where(active, direction, 0.0)
    return (query_grad, key_grad, value_grad, new_moment_one, new_moment_two, weight_step)


def solution(mesh):
    in_specs = (
        P("fsdp", "ctx", "head"),
        P("fsdp", "ctx", "head"),
        P("fsdp", "ctx", "head"),
        P("fsdp", "ctx", "head"),
        P("fsdp", "ctx", "head"),
        P("fsdp", "ctx", "head"),
        P(("ctx", "fsdp"), "head"),
        P(("ctx", "fsdp"), "head"),
        P(("ctx", "fsdp"), "head"),
        P(("ctx", "fsdp")),
        P(),
    )
    out_specs = (
        P("fsdp", "ctx", "head"),
        P("fsdp", "ctx", "head"),
        P("fsdp", "ctx", "head"),
        P(("ctx", "fsdp"), "head"),
        P(("ctx", "fsdp"), "head"),
        P(("ctx", "fsdp"), "head"),
    )
    return jax.shard_map(
        per_device, mesh=mesh, in_specs=in_specs, out_specs=out_specs, check_vma=False
    )
```

```python
import jax
import jax.numpy as jnp
from jax import lax
from jax.sharding import PartitionSpec as P

HEAD_DIM = 128
SPAN = 256
ROW_BLOCK = 32


NORM_EPS = 1e-06
BETA_ONE = 0.9
BETA_TWO = 0.95
ADAM_EPS = 1e-08
WEIGHT_DECAY = 0.1


def window_scan(gain, state, axis, sign):
    count = lax.axis_size(axis)
    place = lax.axis_index(axis)

    def join(near, far):
        return (near[0] * far[0], near[1] + near[0][:, None, None] * far[1])

    def fetch(value, step):
        high = value[0].astype(jnp.bfloat16)
        low = (value[0] - high.astype(jnp.float32)).astype(jnp.bfloat16)
        extra = jnp.broadcast_to(jnp.stack([high, low], axis=1)[:, :, None], (value[1].shape[0], 2, value[1].shape[2]))
        packed = jnp.concatenate([value[1].astype(jnp.bfloat16), extra], axis=1)
        pairs = [(i, i + sign * step) for i in range(count) if 0 <= i + sign * step < count]
        got = lax.ppermute(packed, axis, pairs).astype(jnp.float32)
        rows = value[1].shape[1]
        got = (got[:, rows, 0] + got[:, rows + 1, 0], got[:, :rows])
        source = place - sign * step
        present = (source >= 0) & (source < count)
        return jax.tree.map(lambda g, e: jnp.where(present, g, e), got, identity)

    own = (gain, state)
    identity = (jnp.ones_like(gain), jnp.zeros_like(state))
    total = join(fetch(own, 1), fetch(own, 2))
    step = 2
    while step < count:
        total = join(total, fetch(total, step))
        step *= 2
    return total[1]


def decay_mask(cumul):
    along = jnp.swapaxes(cumul, 1, 2)
    spread = along[:, :, :, None] - along[:, :, None, :]
    length = cumul.shape[1]
    lower = jnp.tril(jnp.ones((length, length), jnp.float32))
    return jnp.exp(jnp.minimum(spread, 0.0)) * lower


def per_device(
    queries,
    keys,
    values,
    gate_pre,
    log_decay,
    out_grad,
    out_weight,
    moment_one,
    moment_two,
    group_ids,
    step_count,
):
    tok_local = queries.shape[1]
    head_local = log_decay.shape[2]
    width_local = queries.shape[2]
    blocks = tok_local // SPAN
    features = lax.all_gather(out_grad, "head", axis=2, tiled=True)[0]
    weight_part = lax.all_gather(out_weight.astype(jnp.bfloat16), "fsdp", axis=0, tiled=True)
    features, weight_part = lax.optimization_barrier((features, weight_part))
    shaped = (blocks, SPAN, head_local, HEAD_DIM)
    query_c = queries.reshape(shaped)
    key_c = keys.reshape(shaped)
    value_c = values.reshape(shaped)
    cumul = jnp.cumsum(log_decay.reshape(blocks, SPAN, head_local), axis=1)
    totals = cumul[:, -1, :]
    masking = decay_mask(cumul)
    decay_in = jnp.exp(cumul)[..., None]
    decay_out = jnp.exp(totals[:, None, :] - cumul)[..., None]
    scores = jnp.einsum("cthe,cuhe->chtu", query_c, key_c, preferred_element_type=jnp.float32)
    probs = (scores * masking).astype(jnp.bfloat16)
    intra = jnp.einsum("chtu,cuhe->cthe", probs, value_c, preferred_element_type=jnp.float32)
    scaled = (decay_out * key_c).astype(jnp.bfloat16)
    updates = jnp.einsum("cthe,cthf->chef", scaled, value_c, preferred_element_type=jnp.float32)
    running = jnp.zeros((head_local, HEAD_DIM, HEAD_DIM), jnp.float32)
    leading = jnp.zeros((head_local,), jnp.float32)
    start_list = []
    lead_list = []
    for block in range(blocks):
        start_list.append(running)
        lead_list.append(leading)
        running = jnp.exp(totals[block])[:, None, None] * running + updates[block]
        leading = leading + totals[block]
    local_start = jnp.stack(start_list)
    lead_sums = jnp.stack(lead_list)
    incoming = window_scan(jnp.exp(leading), running, "ctx", 1)
    states = local_start + jnp.exp(lead_sums)[:, :, None, None] * incoming[None]
    rounded = states.astype(jnp.bfloat16)
    inter = decay_in * jnp.einsum(
        "cthe,chef->cthf", query_c, rounded, preferred_element_type=jnp.float32
    )
    attn = intra + inter
    square = jnp.mean(attn * attn, axis=-1, keepdims=True)
    inverse = lax.rsqrt(square + NORM_EPS)
    normed = attn * inverse
    silu_gate = jax.nn.silu(gate_pre.reshape(shaped).astype(jnp.float32))
    mixed = (normed * silu_gate).astype(jnp.bfloat16).reshape(tok_local, width_local)
    columns = features
    partial = jnp.einsum("td,th->dh", columns, mixed, preferred_element_type=jnp.float32).astype(
        jnp.bfloat16
    )
    weight_full, partial = lax.optimization_barrier(
        (lax.all_gather(weight_part, "ctx", axis=0, tiled=True), partial)
    )
    mixed_grad = jnp.dot(columns, weight_full, preferred_element_type=jnp.float32)
    by_ctx = lax.psum_scatter(partial, "ctx", scatter_dimension=0, tiled=True)
    spread = lax.axis_size("fsdp")
    grad_rows = lax.all_to_all(
        by_ctx.reshape(spread, -1, by_ctx.shape[1]), "fsdp", 0, 0, tiled=False
    ).astype(jnp.float32).sum(0)
    normed_grad = mixed_grad.reshape(shaped) * silu_gate
    inner = jnp.mean(normed_grad * normed, axis=-1, keepdims=True)
    attn_grad = (inverse * (normed_grad - normed * inner)).astype(jnp.bfloat16)
    inners = jnp.einsum("cthf,cuhf->chtu", attn_grad, value_c, preferred_element_type=jnp.float32)
    dprobs = (inners * masking).astype(jnp.bfloat16)
    qgrad = jnp.einsum("chtu,cuhe->cthe", dprobs, key_c, preferred_element_type=jnp.float32)
    kgrad = jnp.einsum("chtu,cthe->cuhe", dprobs, query_c, preferred_element_type=jnp.float32)
    vgrad = jnp.einsum("chtu,cthf->cuhf", probs, attn_grad, preferred_element_type=jnp.float32)
    weighted = (decay_in * query_c).astype(jnp.bfloat16)
    back_updates = jnp.einsum(
        "cthe,cthf->chef", weighted, attn_grad, preferred_element_type=jnp.float32
    )
    backing = jnp.zeros((head_local, HEAD_DIM, HEAD_DIM), jnp.float32)
    trailing = jnp.zeros((head_local,), jnp.float32)
    after_list = [None] * blocks
    trail_list = [None] * blocks
    for block in reversed(range(blocks)):
        after_list[block] = backing
        trail_list[block] = trailing
        backing = jnp.exp(totals[block])[:, None, None] * backing + back_updates[block]
        trailing = trailing + totals[block]
    local_after = jnp.stack(after_list)
    trail_sums = jnp.stack(trail_list)
    arriving = window_scan(jnp.exp(leading), backing, "ctx", -1)
    after_full = local_after + jnp.exp(trail_sums)[:, :, None, None] * arriving[None]
    back_b = after_full.astype(jnp.bfloat16)
    qgrad = qgrad + decay_in * jnp.einsum(
        "cthf,chef->cthe", attn_grad, rounded, preferred_element_type=jnp.float32
    )
    kgrad = kgrad + decay_out * jnp.einsum(
        "cuhf,chef->cuhe", value_c, back_b, preferred_element_type=jnp.float32
    )
    vgrad = vgrad + decay_out * jnp.einsum(
        "cuhe,chef->cuhf", key_c, back_b, preferred_element_type=jnp.float32
    )
    query_grad = qgrad.astype(jnp.bfloat16).reshape(1, tok_local, width_local)
    key_grad = kgrad.astype(jnp.bfloat16).reshape(1, tok_local, width_local)
    value_grad = vgrad.astype(jnp.bfloat16).reshape(1, tok_local, width_local)
    token_count = tok_local * lax.axis_size("ctx") * lax.axis_size("fsdp")
    grad = grad_rows / jnp.sqrt(jnp.float32(token_count))
    row_group = jnp.repeat(group_ids, ROW_BLOCK)[:, None]
    stepped = step_count[0].astype(jnp.float32)
    first = BETA_ONE * moment_one + (1.0 - BETA_ONE) * grad
    second = BETA_TWO * moment_two + (1.0 - BETA_TWO) * grad * grad
    correct_one = 1.0 - jnp.power(BETA_ONE, stepped)
    correct_two = 1.0 - jnp.power(BETA_TWO, stepped)
    active = row_group >= 1
    decayed = (row_group == 2).astype(jnp.float32)
    direction = (
        first / correct_one / (jnp.sqrt(second / correct_two) + ADAM_EPS)
        + WEIGHT_DECAY * decayed * out_weight
    )
    new_moment_one = jnp.where(active, first, moment_one)
    new_moment_two = jnp.where(active, second, moment_two)
    weight_step = jnp.where(active, direction, 0.0)
    return (query_grad, key_grad, value_grad, new_moment_one, new_moment_two, weight_step)


def solution(mesh):
    in_specs = (
        P("fsdp", "ctx", "head"),
        P("fsdp", "ctx", "head"),
        P("fsdp", "ctx", "head"),
        P("fsdp", "ctx", "head"),
        P("fsdp", "ctx", "head"),
        P("fsdp", "ctx", "head"),
        P(("ctx", "fsdp"), "head"),
        P(("ctx", "fsdp"), "head"),
        P(("ctx", "fsdp"), "head"),
        P(("ctx", "fsdp")),
        P(),
    )
    out_specs = (
        P("fsdp", "ctx", "head"),
        P("fsdp", "ctx", "head"),
        P("fsdp", "ctx", "head"),
        P(("ctx", "fsdp"), "head"),
        P(("ctx", "fsdp"), "head"),
        P(("ctx", "fsdp"), "head"),
    )
    return jax.shard_map(
        per_device, mesh=mesh, in_specs=in_specs, out_specs=out_specs, check_vma=False
    )
```
